32 devices in a mesh: groups: 2 (over y), dp: 4 (over z), tensor: 4 (over x, core).
Axes of the slice: x: 2, y: 2, z: 4, core: 2. Of those that a mesh axis runs over, the one named last changes fastest.
Arguments:
- inputs: bfloat16 [2048, 8192], P(('groups', 'dp'), 'tensor'), parts along dimension 0, may hold values from -6 to 6
- cotangent: bfloat16 [2048, 8192], P(('groups', 'dp'), 'tensor'), parts along dimension 0, may hold values from -6 to 6
- up_blocks: bfloat16 [256, 64, 3, 256], P('dp', 'tensor'), may hold values from -0.21875 to 0.21875
- down_blocks: bfloat16 [256, 64, 3, 256], P('dp', 'tensor'), may hold values from -0.15625 to 0.15625
- low_left: bfloat16 [128, 8192], P(None, 'tensor'), may hold values from -0.0625 to 0.0625
- low_right: bfloat16 [128, 16384], P(None, 'tensor'), may hold values from -0.5 to 0.5
- up_pattern: int32 [64, 3], P('tensor'), may hold values from 0 to 7
- down_pattern: int32 [64, 3], P('tensor'), may hold values from 0 to 7
Outputs:
- grad_input: bfloat16 [2048, 8192], P(('groups', 'dp'), 'tensor'), parts along dimension 0
- grad_up: float32 [512, 64, 3, 256], P(('groups', 'dp'), 'tensor'), parts along dimension 0
- grad_down: float32 [512, 64, 3, 256], P(('groups', 'dp'), 'tensor'), parts along dimension 0
- grad_left: float32 [256, 8192], P(('groups', 'dp'), 'tensor'), parts along dimension 0
- grad_right: float32 [256, 16384], P(('groups', 'dp'), 'tensor'), parts along dimension 0
The draws below stay inside these ranges and needn't reach their ends.
There are 2 independent parts, one for each index of `groups`. The reference program is written for one: setup_inputs(seed, part) draws one part's arguments, and reference() takes and returns one part's arrays. A program takes and returns all parts, laid end to end along the dimension named above; an argument that names none is the same for every part. Nothing has to cross between parts.
Inputs may be any that keep to these rules, and one draw needn't show every extreme that they name: `up_pattern`: feature block within a slice of 8 blocks. `down_pattern`: feature block within a slice of 8 blocks.
All inputs are finite; a program needn't handle non-finite values.
Results may differ from the reference program's by a relative error of at most 0.02.
Values may be sent and summed in bfloat16 or wider, within the bound.
No kernel may reach another device: no remote copies, remote signals or barrier semaphores. Data moves between devices by JAX's collectives and lax.ppermute only.
A program may use at most 128 MiB of HBM per device.

```python
import math
import jax
import jax.numpy as jnp
from jax import lax

D = 8192
FF = 16384
BLK = 256
R = 128
SECTIONS = 3
TOK_DEV = 256
TOKENS = 1024
HB = 64
DB_DEV = 8
N_DP = 4
N_TENSOR = 4


def touch_ends(values, own_key, low, top_value):
    longest = values.shape.index(max(values.shape))
    spots = []
    for shift in (0, 1):
        where = [jax.random.randint(jax.random.fold_in(own_key, axis), (), 0, length) for axis, length in enumerate(values.shape)]
        where[longest] = (where[longest] + shift) % values.shape[longest]
        spots.append(tuple(where))
    return values.at[spots[0]].set(low).at[spots[1]].set(top_value)


def steps_of(own_key, shape, pieces, least, largest):
    loudness = 1.0
    for position, parts in pieces:
        heights = jax.random.uniform(jax.random.fold_in(jax.random.fold_in(own_key, 6), position), (parts,), jnp.float32, least / len(pieces), largest / len(pieces))
        loudness = loudness * jnp.repeat(jnp.exp(heights), shape[position] // parts).reshape((-1,) + (1,) * (len(shape) - 1 - position))
    return loudness


def scatter_about(rng, extent, width, reach, split=(), kind=jnp.bfloat16):
    result = width * jax.random.normal(rng, extent, jnp.float32)
    if split:
        result = result * steps_of(rng, extent, split, -0.22, 0.18)
    return jnp.clip(result, -reach, reach).astype(kind)


def setup_inputs(seed: int = 0, part: int = 0) -> dict:
    arg_keys = jax.random.split(jax.random.key(seed), 9)
    own_keys = jax.random.split(jax.random.fold_in(arg_keys[8], part), 9)
    inputs = scatter_about(own_keys[0], (TOKENS, D), 1.0, 6.0, ((0, 4), (1, 4)))
    cotangent = scatter_about(own_keys[1], (TOKENS, D), 1.0, 6.0, ((0, 4), (1, 4)))
    up_blocks = scatter_about(arg_keys[2], (BLK, HB, SECTIONS, BLK), (SECTIONS * BLK) ** -0.5, 0.21875, ((0, 4), (1, 4)))
    down_blocks = scatter_about(arg_keys[3], (BLK, HB, SECTIONS, BLK), (FF * SECTIONS * BLK // D) ** -0.5, 0.15625, ((0, 4), (1, 4)))
    low_left = scatter_about(arg_keys[4], (R, D), D ** -0.5, 0.0625, ((1, 4),))
    low_right = scatter_about(arg_keys[5], (R, FF), R ** -0.5, 0.5, ((1, 4),))
    up_pattern = touch_ends(jax.random.randint(arg_keys[6], (HB, SECTIONS), 0, DB_DEV), jax.random.fold_in(arg_keys[6], 1), 0, DB_DEV - 1).astype(jnp.int32)
    down_pattern = touch_ends(jax.random.randint(arg_keys[7], (HB, SECTIONS), 0, DB_DEV), jax.random.fold_in(arg_keys[7], 1), 0, DB_DEV - 1).astype(jnp.int32)
    return {"inputs": inputs, "cotangent": cotangent, "up_blocks": up_blocks, "down_blocks": down_blocks, "low_left": low_left, "low_right": low_right, "up_pattern": up_pattern, "down_pattern": down_pattern}


root_coef = 0.7978845608028654
cubic_coef = 0.044715

def gelu_pair(values):
    inner_arg = root_coef * (values + cubic_coef * values * values * values)
    tangent = jnp.tanh(inner_arg)
    forward = 0.5 * values * (1.0 + tangent)
    slopes = 0.5 * (1.0 + tangent) + 0.5 * values * (1.0 - tangent * tangent) * root_coef * (1.0 + 3.0 * cubic_coef * values * values)
    return (forward, slopes)

def round_trip(values):
    narrow = lax.optimization_barrier(values.astype(jnp.bfloat16))
    return narrow.astype(jnp.float32)

def reference(inputs, cotangent, up_blocks, down_blocks, low_left, low_right, up_pattern, down_pattern):
    block_dev = D // (BLK * N_TENSOR)
    hidden_dev = FF // (BLK * N_TENSOR)
    hidden_all = FF // BLK
    block_all = D // BLK
    owners = jnp.arange(hidden_all, dtype=jnp.int32) // hidden_dev
    xor_masks = jnp.array([0] + [1 << level_bit for level_bit in range(SECTIONS - 1)], dtype=jnp.int32)
    sources = jnp.bitwise_xor(owners[:, None], xor_masks[None, :])
    up_index = (sources * block_dev + up_pattern).astype(jnp.int32)
    down_index = (owners[:, None] * block_dev + down_pattern).astype(jnp.int32)
    block_ids = jnp.arange(block_all, dtype=jnp.int32)
    onehot = (up_index[:, :, None] == block_ids[None, None, :]).astype(jnp.float32)
    up_float = up_blocks.astype(jnp.float32)
    down_float = down_blocks.astype(jnp.float32)
    inv_root = 1.0 / math.sqrt(TOKENS)

    def one_run(totals, run_pair):
        run_inputs, run_cotangent = run_pair
        selected = run_inputs.astype(jnp.float32).reshape(TOK_DEV, block_all, BLK)[:, up_index, :]
        sparse = jnp.einsum('thsi,ihsj->thj', selected, up_float)
        low_sum = jnp.dot(run_inputs, low_left.T, preferred_element_type=jnp.float32)
        low_narrow = low_sum.astype(jnp.bfloat16)
        preact = sparse.reshape(TOK_DEV, FF) + jnp.dot(low_narrow, low_right, preferred_element_type=jnp.float32)
        activated, slopes = gelu_pair(preact)
        hidden = activated.astype(jnp.bfloat16)
        picked = run_cotangent.astype(jnp.float32).reshape(TOK_DEV, block_all, BLK)[:, down_index, :]
        grad_hidden = jnp.einsum('thso,jhso->thj', picked, down_float).reshape(TOK_DEV, FF)
        grad_pre = (grad_hidden * slopes).astype(jnp.bfloat16)
        grad_blocks = grad_pre.astype(jnp.float32).reshape(TOK_DEV, hidden_all, BLK)
        spread = jnp.einsum('thj,ihsj->thsi', grad_blocks, up_float)
        section_terms = jnp.einsum('thsi,hsd->tsdi', spread, onehot)
        own_term = section_terms[:, 0].reshape(TOK_DEV, D)
        partner_terms = lax.optimization_barrier(jnp.sum(round_trip(section_terms[:, 1:]), axis=1)).reshape(TOK_DEV, D)
        back_low = jnp.dot(grad_pre, low_right.T, preferred_element_type=jnp.float32)
        back_narrow = back_low.astype(jnp.bfloat16)
        low_grad = jnp.dot(back_narrow, low_left, preferred_element_type=jnp.float32)
        grad_rows = (own_term + partner_terms + low_grad).astype(jnp.bfloat16)
        part_up = round_trip(jnp.einsum('thsi,thj->ihsj', selected, grad_blocks) * inv_root)
        hidden_blocks = hidden.astype(jnp.float32).reshape(TOK_DEV, hidden_all, BLK)
        part_down = round_trip(jnp.einsum('thj,thso->jhso', hidden_blocks, picked) * inv_root)
        part_left = round_trip(jnp.dot(back_narrow.T, run_inputs, preferred_element_type=jnp.float32) * inv_root)
        part_right = round_trip(jnp.dot(low_narrow.T, grad_pre, preferred_element_type=jnp.float32) * inv_root)
        new_totals = (totals[0] + part_up, totals[1] + part_down, totals[2] + part_left, totals[3] + part_right)
        return (new_totals, grad_rows)
    start_totals = (jnp.zeros((BLK, hidden_all, SECTIONS, BLK), jnp.float32), jnp.zeros((BLK, hidden_all, SECTIONS, BLK), jnp.float32), jnp.zeros((R, D), jnp.float32), jnp.zeros((R, FF), jnp.float32))
    run_inputs_all = inputs.reshape(N_DP, TOK_DEV, D)
    run_cotangent_all = cotangent.reshape(N_DP, TOK_DEV, D)
    totals, grad_runs = lax.scan(one_run, start_totals, (run_inputs_all, run_cotangent_all))
    grad_input = grad_runs.reshape(TOKENS, D)
    return (grad_input, totals[0], totals[1], totals[2], totals[3])
```

```python
import math

import jax
import jax.numpy as jnp
from jax import lax
from jax.sharding import PartitionSpec as P

root_coef = 0.7978845608028654
cubic_coef = 0.044715


def swapped(block, axis, distance):
    count = lax.axis_size(axis)
    route = []
    for low in range(count):
        high = low | 1 << distance
        if high != low and high < count:
            route += [(low, high), (high, low)]
    return lax.ppermute(block, axis, route)


def line_gather(block, axis):
    count = lax.axis_size(axis)
    if count == 1:
        return block
    if count > 8:
        return lax.all_gather(block, axis, axis=0, tiled=True)
    me = lax.axis_index(axis)
    from_left, from_right = [], []
    rightward = leftward = block
    for step in range(1, count):
        rightward = lax.ppermute(rightward, axis, [(i, i + 1) for i in range(step - 1, count - 1)])
        leftward = lax.ppermute(leftward, axis, [(i + 1, i) for i in range(0, count - step)])
        from_left.append(rightward)
        from_right.append(leftward)
    window = jnp.concatenate(from_left[::-1] + [block] + from_right, axis=0)
    rows = block.shape[0]
    return lax.dynamic_slice_in_dim(window, (count - 1 - me) * rows, count * rows, axis=0)


def gelu_pair(values):
    inner_arg = root_coef * (values + cubic_coef * values * values * values)
    tangent = jnp.tanh(inner_arg)
    forward = 0.5 * values * (1.0 + tangent)
    slopes = 0.5 * (1.0 + tangent) + 0.5 * values * (1.0 - tangent * tangent) * root_coef * (
        1.0 + 3.0 * cubic_coef * values * values
    )
    return (forward, slopes)


def pick_blocks(slices, pattern, block_size):
    picked = []
    for which_section, source in enumerate(slices):
        shaped = source.reshape(source.shape[0], -1, block_size)
        picked.append(jnp.take(shaped, pattern[:, which_section], axis=1))
    return jnp.stack(picked, axis=2)


def scatter_dp(parts, inv_root, after=None):
    narrow = (jnp.stack(parts) * inv_root).astype(jnp.bfloat16)
    if after is not None:
        narrow, _ = lax.optimization_barrier((narrow, after))
    return lax.psum_scatter(narrow, "dp", scatter_dimension=0, tiled=False).astype(jnp.float32)


def row_split(values, axis):
    count = lax.axis_size("dp")
    rows = values.shape[axis] // count
    return [lax.slice_in_dim(values, d * rows, (d + 1) * rows, axis=axis) for d in range(count)]


def shards(
    inputs, cotangent, up_blocks, down_blocks, low_left, low_right, up_pattern, down_pattern
):
    tokens_here, width_here = inputs.shape
    block_size = up_blocks.shape[3]
    hidden_here = up_blocks.shape[1]
    section_count = up_blocks.shape[2]
    blocks_here = width_here // block_size
    dp_size = lax.axis_size("dp")
    inv_root = 1.0 / math.sqrt(tokens_here * dp_size)
    chunk_count = 4 if hidden_here % 4 == 0 else 1
    per_chunk = hidden_here // chunk_count
    width_chunk = per_chunk * block_size

    sources = [inputs] + [
        swapped(inputs, "tensor", level_bit) for level_bit in range(section_count - 1)
    ]
    selected = pick_blocks(sources, up_pattern, block_size)
    picked = pick_blocks([cotangent] * section_count, down_pattern, block_size)
    low_part = lax.dot_general(
        inputs, low_left, (((1,), (1,)), ((), ())), preferred_element_type=jnp.float32
    )
    low_sum = lax.psum(low_part.astype(jnp.bfloat16), "tensor")
    slot_ids = jnp.arange(blocks_here, dtype=jnp.int32)

    terms = [None] * section_count
    back_part = None
    grad_pre_chunks, grad_up_chunks, grad_down_chunks = [], [], []
    for chunk in range(chunk_count):
        lo = chunk * per_chunk
        hi = lo + per_chunk
        up_full = line_gather(up_blocks[:, lo:hi], "dp")
        down_full = line_gather(down_blocks[:, lo:hi], "dp")
        selected_here = selected[:, lo:hi]
        picked_here = picked[:, lo:hi]
        sparse = jnp.einsum(
            "thsi,ihsj->thj", selected_here, up_full, preferred_element_type=jnp.float32
        )
        preact = sparse.reshape(tokens_here, -1) + jnp.dot(
            low_sum,
            low_right[:, lo * block_size : hi * block_size],
            preferred_element_type=jnp.float32,
        )
        activated, slopes = gelu_pair(preact)
        hidden = activated.astype(jnp.bfloat16)
        grad_hidden = jnp.einsum(
            "thso,jhso->thj", picked_here, down_full, preferred_element_type=jnp.float32
        ).reshape(tokens_here, -1)
        grad_pre = (grad_hidden * slopes).astype(jnp.bfloat16)
        grad_pre_chunks.append(grad_pre)
        grad_blocks = grad_pre.reshape(tokens_here, per_chunk, block_size)
        for which_section in range(section_count):
            spread = jnp.einsum(
                "thj,ihj->thi",
                grad_blocks,
                up_full[:, :, which_section, :],
                preferred_element_type=jnp.float32,
            )
            placing = (
                up_pattern[lo:hi, which_section][:, None] == slot_ids[None, :]
            ).astype(jnp.float32)
            term = jnp.einsum("thi,hd->tdi", spread, placing).reshape(tokens_here, width_here)
            terms[which_section] = term if terms[which_section] is None else terms[which_section] + term
        back_here = lax.dot_general(
            grad_pre,
            low_right[:, lo * block_size : hi * block_size],
            (((1,), (1,)), ((), ())),
            preferred_element_type=jnp.float32,
        )
        back_part = back_here if back_part is None else back_part + back_here
        grad_up_chunks.append(
            scatter_dp(
                [
                    jnp.einsum("thsi,thj->hsij", rows, grad_blocks, preferred_element_type=jnp.float32)
                    for rows in row_split(selected_here, 3)
                ],
                inv_root,
                grad_down_chunks[-1] if grad_down_chunks else None,
            )
        )
        hidden_blocks = hidden.reshape(tokens_here, per_chunk, block_size)
        grad_down_chunks.append(
            scatter_dp(
                [
                    jnp.einsum("thj,thso->hjso", rows, picked_here, preferred_element_type=jnp.float32)
                    for rows in row_split(hidden_blocks, 2)
                ],
                inv_root,
                grad_up_chunks[-1],
            )
        )

    own_term = terms[0]
    for level_bit in range(section_count - 1):
        outgoing = terms[level_bit + 1].astype(jnp.bfloat16)
        own_term = own_term + swapped(outgoing, "tensor", level_bit).astype(jnp.float32)
    back_low = lax.psum(back_part.astype(jnp.bfloat16), "tensor")
    grad_input = (
        own_term + jnp.dot(back_low, low_left, preferred_element_type=jnp.float32)
    ).astype(jnp.bfloat16)
    grad_pre_all = jnp.concatenate(grad_pre_chunks, axis=1)
    grad_up = jnp.transpose(jnp.concatenate(grad_up_chunks, axis=0), (2, 0, 1, 3))
    grad_down = jnp.transpose(jnp.concatenate(grad_down_chunks, axis=0), (1, 0, 2, 3))
    grad_left = scatter_dp(
        row_split(
            lax.dot_general(
                back_low, inputs, (((0,), (0,)), ((), ())), preferred_element_type=jnp.float32
            ),
            0,
        ),
        inv_root,
    )
    grad_right = scatter_dp(
        row_split(
            lax.dot_general(
                low_sum, grad_pre_all, (((0,), (0,)), ((), ())), preferred_element_type=jnp.float32
            ),
            0,
        ),
        inv_root,
    )
    return (grad_input, grad_up, grad_down, grad_left, grad_right)


def solution(mesh):
    in_specs = (
        P(("groups", "dp"), "tensor"),
        P(("groups", "dp"), "tensor"),
        P("dp", "tensor", None, None),
        P("dp", "tensor", None, None),
        P(None, "tensor"),
        P(None, "tensor"),
        P("tensor", None),
        P("tensor", None),
    )
    out_specs = (
        P(("groups", "dp"), "tensor"),
        P(("groups", "dp"), "tensor", None, None),
        P(("groups", "dp"), "tensor", None, None),
        P(("groups", "dp"), "tensor"),
        P(("groups", "dp"), "tensor"),
    )
    return jax.shard_map(shards, mesh=mesh, in_specs=in_specs, out_specs=out_specs, check_vma=False)
```

```python
import math

import jax
import jax.numpy as jnp
from jax import lax
from jax.sharding import PartitionSpec as P

root_coef = 0.7978845608028654
cubic_coef = 0.044715


def swapped(block, axis, distance):
    count = lax.axis_size(axis)
    route = []
    for low in range(count):
        high = low | 1 << distance
        if high != low and high < count:
            route += [(low, high), (high, low)]
    return lax.ppermute(block, axis, route)


def shared_gather(block):
    group_count = lax.axis_size("groups")
    dp_count = lax.axis_size("dp")
    rows = block.shape[0]
    if group_count == 1 or rows % group_count:
        return lax.all_gather(block, "dp", axis=0, tiled=True)
    share = rows // group_count
    mine = lax.dynamic_slice_in_dim(block, lax.axis_index("groups") * share, share, axis=0)
    gathered = lax.all_gather(mine, ("groups", "dp"), axis=0, tiled=True)
    rest = block.shape[1:]
    gathered = gathered.reshape((group_count, dp_count, share) + rest)
    gathered = jnp.swapaxes(gathered, 0, 1)
    return gathered.reshape((dp_count * rows,) + rest)


def butterfly_sum(values, axis):
    count = lax.axis_size(axis)
    if count & (count - 1):
        return lax.psum(values.astype(jnp.bfloat16), axis).astype(jnp.float32)
    total = values
    distance = 0
    while (1 << distance) < count:
        total = total + swapped(total, axis, distance)
        distance += 1
    return total


def gelu_pair(values):
    inner_arg = root_coef * (values + cubic_coef * values * values * values)
    tangent = jnp.tanh(inner_arg)
    forward = 0.5 * values * (1.0 + tangent)
    slopes = 0.5 * (1.0 + tangent) + 0.5 * values * (1.0 - tangent * tangent) * root_coef * (
        1.0 + 3.0 * cubic_coef * values * values
    )
    return (forward, slopes)


def pick_blocks(slices, pattern, block_size):
    picked = []
    for which_section, source in enumerate(slices):
        shaped = source.reshape(source.shape[0], -1, block_size)
        picked.append(jnp.take(shaped, pattern[:, which_section], axis=1))
    return jnp.stack(picked, axis=2)


def shards(
    inputs, cotangent, up_blocks, down_blocks, low_left, low_right, up_pattern, down_pattern
):
    tokens_here, width_here = inputs.shape
    block_size = up_blocks.shape[3]
    hidden_here = up_blocks.shape[1]
    section_count = up_blocks.shape[2]
    blocks_here = width_here // block_size
    dp_size = lax.axis_size("dp")
    inv_root = 1.0 / math.sqrt(tokens_here * dp_size)
    up_full, down_full = (shared_gather(up_blocks), shared_gather(down_blocks))
    sources = [inputs] + [
        swapped(inputs, "tensor", level_bit) for level_bit in range(section_count - 1)
    ]
    selected = pick_blocks(sources, up_pattern, block_size)
    sparse = jnp.einsum("thsi,ihsj->thj", selected, up_full, preferred_element_type=jnp.float32)
    low_part = lax.dot_general(
        inputs, low_left, (((1,), (1,)), ((), ())), preferred_element_type=jnp.float32
    )
    low_sum = butterfly_sum(low_part, "tensor").astype(jnp.bfloat16)
    preact = sparse.reshape(tokens_here, -1) + jnp.dot(
        low_sum, low_right, preferred_element_type=jnp.float32
    )
    activated, slopes = gelu_pair(preact)
    hidden = activated.astype(jnp.bfloat16)
    picked = pick_blocks([cotangent] * section_count, down_pattern, block_size)
    grad_hidden = jnp.einsum(
        "thso,jhso->thj", picked, down_full, preferred_element_type=jnp.float32
    ).reshape(tokens_here, -1)
    grad_pre = (grad_hidden * slopes).astype(jnp.bfloat16)
    grad_blocks = grad_pre.reshape(tokens_here, hidden_here, block_size)
    slot_ids = jnp.arange(blocks_here, dtype=jnp.int32)

    def section_term(which_section):
        spread = jnp.einsum(
            "thj,ihj->thi",
            grad_blocks,
            up_full[:, :, which_section, :],
            preferred_element_type=jnp.float32,
        )
        placing = (up_pattern[:, which_section][:, None] == slot_ids[None, :]).astype(jnp.float32)
        return jnp.einsum("thi,hd->tdi", spread, placing).reshape(tokens_here, width_here)

    own_term = section_term(0)
    for level_bit in range(section_count - 1):
        outgoing = section_term(level_bit + 1).astype(jnp.bfloat16)
        own_term = own_term + swapped(outgoing, "tensor", level_bit).astype(jnp.float32)
    back_part = lax.dot_general(
        grad_pre, low_right, (((1,), (1,)), ((), ())), preferred_element_type=jnp.float32
    )
    back_low = butterfly_sum(back_part, "tensor").astype(jnp.bfloat16)
    grad_input = (
        own_term + jnp.dot(back_low, low_left, preferred_element_type=jnp.float32)
    ).astype(jnp.bfloat16)
    row_part = selected
    grad_up = lax.psum_scatter(
        (
            jnp.einsum("thsi,thj->ihsj", row_part, grad_blocks, preferred_element_type=jnp.float32)
            * inv_root
        ).astype(jnp.bfloat16),
        "dp",
        scatter_dimension=0,
        tiled=True,
    ).astype(jnp.float32)
    hidden_blocks = hidden.reshape(tokens_here, hidden_here, block_size)
    row_part = hidden_blocks
    grad_down = lax.psum_scatter(
        (
            jnp.einsum("thj,thso->jhso", row_part, picked, preferred_element_type=jnp.float32)
            * inv_root
        ).astype(jnp.bfloat16),
        "dp",
        scatter_dimension=0,
        tiled=True,
    ).astype(jnp.float32)
    row_part = back_low
    grad_left = lax.psum_scatter(
        (
            lax.dot_general(
                row_part, inputs, (((0,), (0,)), ((), ())), preferred_element_type=jnp.float32
            )
            * inv_root
        ).astype(jnp.bfloat16),
        "dp",
        scatter_dimension=0,
        tiled=True,
    ).astype(jnp.float32)
    row_part = low_sum
    grad_right = lax.psum_scatter(
        (
            lax.dot_general(
                row_part, grad_pre, (((0,), (0,)), ((), ())), preferred_element_type=jnp.float32
            )
            * inv_root
        ).astype(jnp.bfloat16),
        "dp",
        scatter_dimension=0,
        tiled=True,
    ).astype(jnp.float32)
    return (grad_input, grad_up, grad_down, grad_left, grad_right)


def solution(mesh):
    in_specs = (
        P(("groups", "dp"), "tensor"),
        P(("groups", "dp"), "tensor"),
        P("dp", "tensor", None, None),
        P("dp", "tensor", None, None),
        P(None, "tensor"),
        P(None, "tensor"),
        P("tensor", None),
        P("tensor", None),
    )
    out_specs = (
        P(("groups", "dp"), "tensor"),
        P(("groups", "dp"), "tensor", None, None),
        P(("groups", "dp"), "tensor", None, None),
        P(("groups", "dp"), "tensor"),
        P(("groups", "dp"), "tensor"),
    )
    return jax.shard_map(shards, mesh=mesh, in_specs=in_specs, out_specs=out_specs, check_vma=False)
```

```python
import math

import jax
import jax.numpy as jnp
from jax import lax
from jax.sharding import PartitionSpec as P

root_coef = 0.7978845608028654
cubic_coef = 0.044715


def swapped(block, axis, distance):
    count = lax.axis_size(axis)
    route = []
    for low in range(count):
        high = low | 1 << distance
        if high != low and high < count:
            route += [(low, high), (high, low)]
    return lax.ppermute(block, axis, route)


def shared_gather(block, after=None):
    group_count = lax.axis_size("groups")
    dp_count = lax.axis_size("dp")
    rows = block.shape[0]
    if group_count == 1 or rows % group_count:
        return lax.all_gather(block, "dp", axis=0, tiled=True)
    share = rows // group_count
    mine = lax.dynamic_slice_in_dim(block, lax.axis_index("groups") * share, share, axis=0)
    if after is not None:
        mine, _ = lax.optimization_barrier((mine, after))
    return lax.all_gather(mine, ("dp", "groups"), axis=0, tiled=True)


def line_scatter(parts, axis):
    count = lax.axis_size(axis)
    if count > 8:
        return lax.psum_scatter(parts, axis, scatter_dimension=0, tiled=False).astype(jnp.float32)
    me = lax.axis_index(axis)
    own = lax.dynamic_index_in_dim(parts, me, 0, keepdims=False).astype(jnp.float32)
    if count == 1:
        return own
    rightward = leftward = None
    for step in range(1, count):
        ahead = lax.dynamic_index_in_dim(
            parts, jnp.clip(me + count - step, 0, count - 1), 0, keepdims=False
        ).astype(jnp.float32)
        behind = lax.dynamic_index_in_dim(
            parts, jnp.clip(me - count + step, 0, count - 1), 0, keepdims=False
        ).astype(jnp.float32)
        if rightward is not None:
            ahead = ahead + rightward.astype(jnp.float32)
            behind = behind + leftward.astype(jnp.float32)
        rightward = lax.ppermute(
            ahead.astype(jnp.bfloat16), axis, [(i, i + 1) for i in range(0, min(step, count - 1))]
        )
        leftward = lax.ppermute(
            behind.astype(jnp.bfloat16), axis, [(i, i - 1) for i in range(max(count - step, 1), count)]
        )
    return own + rightward.astype(jnp.float32) + leftward.astype(jnp.float32)


def split_rows(values, axis, count):
    rows = values.shape[axis] // count
    return [lax.slice_in_dim(values, d * rows, (d + 1) * rows, axis=axis) for d in range(count)]


def butterfly_sum(values, axis):
    count = lax.axis_size(axis)
    if count & (count - 1):
        return lax.psum(values.astype(jnp.bfloat16), axis).astype(jnp.float32)
    total = values
    distance = 0
    while (1 << distance) < count:
        total = total + swapped(total, axis, distance)
        distance += 1
    return total


def gelu_pair(values):
    inner_arg = root_coef * (values + cubic_coef * values * values * values)
    tangent = jnp.tanh(inner_arg)
    forward = 0.5 * values * (1.0 + tangent)
    slopes = 0.5 * (1.0 + tangent) + 0.5 * values * (1.0 - tangent * tangent) * root_coef * (
        1.0 + 3.0 * cubic_coef * values * values
    )
    return (forward, slopes)


def pick_blocks(slices, pattern, block_size):
    picked = []
    for which_section, source in enumerate(slices):
        shaped = source.reshape(source.shape[0], -1, block_size)
        picked.append(jnp.take(shaped, pattern[:, which_section], axis=1))
    return jnp.stack(picked, axis=2)


def shards(
    inputs, cotangent, up_blocks, down_blocks, low_left, low_right, up_pattern, down_pattern
):
    tokens_here, width_here = inputs.shape
    block_size = up_blocks.shape[3]
    hidden_here = up_blocks.shape[1]
    section_count = up_blocks.shape[2]
    blocks_here = width_here // block_size
    dp_size = lax.axis_size("dp")
    inv_root = 1.0 / math.sqrt(tokens_here * dp_size)
    up_full = shared_gather(up_blocks)
    sources = [inputs] + [
        swapped(inputs, "tensor", level_bit) for level_bit in range(section_count - 1)
    ]
    selected = pick_blocks(sources, up_pattern, block_size)
    sparse = jnp.einsum("thsi,ihsj->thj", selected, up_full, preferred_element_type=jnp.float32)
    low_part = lax.dot_general(
        inputs, low_left, (((1,), (1,)), ((), ())), preferred_element_type=jnp.float32
    )
    low_sum = butterfly_sum(low_part, "tensor").astype(jnp.bfloat16)
    preact = sparse.reshape(tokens_here, -1) + jnp.dot(
        low_sum, low_right, preferred_element_type=jnp.float32
    )
    activated, slopes = gelu_pair(preact)
    hidden = activated.astype(jnp.bfloat16)
    picked = pick_blocks([cotangent] * section_count, down_pattern, block_size)
    down_full = shared_gather(down_blocks, hidden)
    hidden_blocks = hidden.reshape(tokens_here, hidden_here, block_size)
    grad_down = line_scatter(
        (
            jnp.stack(
                [
                    jnp.einsum("thj,thso->hjso", rows, picked, preferred_element_type=jnp.float32)
                    for rows in split_rows(hidden_blocks, 2, dp_size)
                ]
            )
            * inv_root
        ).astype(jnp.bfloat16),
        "dp",
    )
    grad_down = jnp.transpose(grad_down, (1, 0, 2, 3))
    down_full, grad_down = lax.optimization_barrier((down_full, grad_down))
    grad_hidden = jnp.einsum(
        "thso,jhso->thj", picked, down_full, preferred_element_type=jnp.float32
    ).reshape(tokens_here, -1)
    grad_pre = (grad_hidden * slopes).astype(jnp.bfloat16)
    grad_blocks = grad_pre.reshape(tokens_here, hidden_here, block_size)
    grad_up = lax.psum_scatter(
        (
            jnp.stack(
                [
                    jnp.einsum("thsi,thj->hsij", rows, grad_blocks, preferred_element_type=jnp.float32)
                    for rows in split_rows(selected, 3, dp_size)
                ]
            )
            * inv_root
        ).astype(jnp.bfloat16),
        "dp",
        scatter_dimension=0,
        tiled=False,
    ).astype(jnp.float32)
    grad_up = jnp.transpose(grad_up, (2, 0, 1, 3))
    slot_ids = jnp.arange(blocks_here, dtype=jnp.int32)

    def section_term(which_section):
        spread = jnp.einsum(
            "thj,ihj->thi",
            grad_blocks,
            up_full[:, :, which_section, :],
            preferred_element_type=jnp.float32,
        )
        placing = (up_pattern[:, which_section][:, None] == slot_ids[None, :]).astype(jnp.float32)
        return jnp.einsum("thi,hd->tdi", spread, placing).reshape(tokens_here, width_here)

    own_term = section_term(0)
    for level_bit in range(section_count - 1):
        outgoing = section_term(level_bit + 1).astype(jnp.bfloat16)
        own_term = own_term + swapped(outgoing, "tensor", level_bit).astype(jnp.float32)
    back_part = lax.dot_general(
        grad_pre, low_right, (((1,), (1,)), ((), ())), preferred_element_type=jnp.float32
    )
    back_low = butterfly_sum(back_part, "tensor").astype(jnp.bfloat16)
    grad_input = (
        own_term + jnp.dot(back_low, low_left, preferred_element_type=jnp.float32)
    ).astype(jnp.bfloat16)
    row_part, low_row_part, grad_up = lax.optimization_barrier((back_low, low_sum, grad_up))
    grad_left = lax.psum_scatter(
        (
            lax.dot_general(
                row_part, inputs, (((0,), (0,)), ((), ())), preferred_element_type=jnp.float32
            )
            * inv_root
        ).astype(jnp.bfloat16),
        "dp",
        scatter_dimension=0,
        tiled=True,
    ).astype(jnp.float32)
    row_part = low_row_part
    grad_right = lax.psum_scatter(
        (
            lax.dot_general(
                row_part, grad_pre, (((0,), (0,)), ((), ())), preferred_element_type=jnp.float32
            )
            * inv_root
        ).astype(jnp.bfloat16),
        "dp",
        scatter_dimension=0,
        tiled=True,
    ).astype(jnp.float32)
    return (grad_input, grad_up, grad_down, grad_left, grad_right)


def solution(mesh):
    in_specs = (
        P(("groups", "dp"), "tensor"),
        P(("groups", "dp"), "tensor"),
        P("dp", "tensor", None, None),
        P("dp", "tensor", None, None),
        P(None, "tensor"),
        P(None, "tensor"),
        P("tensor", None),
        P("tensor", None),
    )
    out_specs = (
        P(("groups", "dp"), "tensor"),
        P(("groups", "dp"), "tensor", None, None),
        P(("groups", "dp"), "tensor", None, None),
        P(("groups", "dp"), "tensor"),
        P(("groups", "dp"), "tensor"),
    )
    return jax.shard_map(shards, mesh=mesh, in_specs=in_specs, out_specs=out_specs, check_vma=False)
```

```python
import math

import jax
import jax.numpy as jnp
from jax import lax
from jax.sharding import PartitionSpec as P

root_coef = 0.7978845608028654
cubic_coef = 0.044715


def swapped(block, axis, distance):
    count = lax.axis_size(axis)
    route = []
    for low in range(count):
        high = low | 1 << distance
        if high != low and high < count:
            route += [(low, high), (high, low)]
    return lax.ppermute(block, axis, route)


def shared_gather(block, after=None):
    group_count = lax.axis_size("groups")
    dp_count = lax.axis_size("dp")
    rows = block.shape[0]
    if group_count == 1 or rows % group_count:
        return lax.all_gather(block, "dp", axis=0, tiled=True)
    share = rows // group_count
    mine = lax.dynamic_slice_in_dim(block, lax.axis_index("groups") * share, share, axis=0)
    if after is not None:
        mine, _ = lax.optimization_barrier((mine, after))
    return lax.all_gather(mine, ("dp", "groups"), axis=0, tiled=True)


def split_rows(values, axis, count):
    rows = values.shape[axis] // count
    return [lax.slice_in_dim(values, d * rows, (d + 1) * rows, axis=axis) for d in range(count)]


def butterfly_sum(values, axis):
    count = lax.axis_size(axis)
    if count & (count - 1):
        return lax.psum(values.astype(jnp.bfloat16), axis).astype(jnp.float32)
    total = values
    distance = 0
    while (1 << distance) < count:
        total = total + swapped(total, axis, distance)
        distance += 1
    return total


def gelu_pair(values):
    inner_arg = root_coef * (values + cubic_coef * values * values * values)
    tangent = jnp.tanh(inner_arg)
    forward = 0.5 * values * (1.0 + tangent)
    slopes = 0.5 * (1.0 + tangent) + 0.5 * values * (1.0 - tangent * tangent) * root_coef * (
        1.0 + 3.0 * cubic_coef * values * values
    )
    return (forward, slopes)


def pick_blocks(slices, pattern, block_size):
    picked = []
    for which_section, source in enumerate(slices):
        shaped = source.reshape(source.shape[0], -1, block_size)
        picked.append(jnp.take(shaped, pattern[:, which_section], axis=1))
    return jnp.stack(picked, axis=2)


def shards(
    inputs, cotangent, up_blocks, down_blocks, low_left, low_right, up_pattern, down_pattern
):
    tokens_here, width_here = inputs.shape
    block_size = up_blocks.shape[3]
    hidden_here = up_blocks.shape[1]
    section_count = up_blocks.shape[2]
    blocks_here = width_here // block_size
    dp_size = lax.axis_size("dp")
    inv_root = 1.0 / math.sqrt(tokens_here * dp_size)
    up_full = shared_gather(up_blocks)
    down_full = shared_gather(down_blocks)
    sources = [inputs] + [
        swapped(inputs, "tensor", level_bit) for level_bit in range(section_count - 1)
    ]
    selected = pick_blocks(sources, up_pattern, block_size)
    sparse = jnp.einsum("thsi,ihsj->thj", selected, up_full, preferred_element_type=jnp.float32)
    low_part = lax.dot_general(
        inputs, low_left, (((1,), (1,)), ((), ())), preferred_element_type=jnp.float32
    )
    low_sum = butterfly_sum(low_part, "tensor").astype(jnp.bfloat16)
    preact = sparse.reshape(tokens_here, -1) + jnp.dot(
        low_sum, low_right, preferred_element_type=jnp.float32
    )
    activated, slopes = gelu_pair(preact)
    hidden = activated.astype(jnp.bfloat16)
    picked = pick_blocks([cotangent] * section_count, down_pattern, block_size)
    hidden_blocks = hidden.reshape(tokens_here, hidden_here, block_size)
    down_parts = (
        jnp.stack(
            [
                jnp.einsum("thj,thso->hjso", rows, picked, preferred_element_type=jnp.float32)
                for rows in split_rows(hidden_blocks, 2, dp_size)
            ]
        )
        * inv_root
    ).astype(jnp.bfloat16)
    down_parts, down_full = lax.optimization_barrier((down_parts, down_full))
    grad_down = lax.psum_scatter(
        down_parts, "dp", scatter_dimension=0, tiled=False
    ).astype(jnp.float32)
    grad_down = jnp.transpose(grad_down, (1, 0, 2, 3))
    grad_hidden = jnp.einsum(
        "thso,jhso->thj", picked, down_full, preferred_element_type=jnp.float32
    ).reshape(tokens_here, -1)
    grad_pre = (grad_hidden * slopes).astype(jnp.bfloat16)
    grad_blocks = grad_pre.reshape(tokens_here, hidden_here, block_size)
    up_parts = jnp.stack(
        [
            jnp.einsum("thsi,thj->hsij", rows, grad_blocks, preferred_element_type=jnp.float32)
            for rows in split_rows(selected, 3, dp_size)
        ]
    )
    slot_ids = jnp.arange(blocks_here, dtype=jnp.int32)

    def section_term(which_section):
        spread = jnp.einsum(
            "thj,ihj->thi",
            grad_blocks,
            up_full[:, :, which_section, :],
            preferred_element_type=jnp.float32,
        )
        placing = (up_pattern[:, which_section][:, None] == slot_ids[None, :]).astype(jnp.float32)
        return jnp.einsum("thi,hd->tdi", spread, placing).reshape(tokens_here, width_here)

    own_term = section_term(0)
    for level_bit in range(section_count - 1):
        outgoing = section_term(level_bit + 1).astype(jnp.bfloat16)
        own_term = own_term + swapped(outgoing, "tensor", level_bit).astype(jnp.float32)
    back_part = lax.dot_general(
        grad_pre, low_right, (((1,), (1,)), ((), ())), preferred_element_type=jnp.float32
    )
    back_low = butterfly_sum(back_part, "tensor").astype(jnp.bfloat16)
    grad_input = (
        own_term + jnp.dot(back_low, low_left, preferred_element_type=jnp.float32)
    ).astype(jnp.bfloat16)
    up_parts, _ = lax.optimization_barrier((up_parts, grad_down))
    grad_up = lax.psum_scatter(
        (up_parts * inv_root).astype(jnp.bfloat16), "dp", scatter_dimension=0, tiled=False
    ).astype(jnp.float32)
    row_part, low_row_part, grad_up = lax.optimization_barrier((back_low, low_sum, grad_up))
    grad_up = jnp.transpose(grad_up, (2, 0, 1, 3))
    grad_left = lax.psum_scatter(
        (
            lax.dot_general(
                row_part, inputs, (((0,), (0,)), ((), ())), preferred_element_type=jnp.float32
            )
            * inv_root
        ).astype(jnp.bfloat16),
        "dp",
        scatter_dimension=0,
        tiled=True,
    ).astype(jnp.float32)
    grad_right = lax.psum_scatter(
        (
            lax.dot_general(
                low_row_part, grad_pre, (((0,), (0,)), ((), ())), preferred_element_type=jnp.float32
            )
            * inv_root
        ).astype(jnp.bfloat16),
        "dp",
        scatter_dimension=0,
        tiled=True,
    ).astype(jnp.float32)
    return (grad_input, grad_up, grad_down, grad_left, grad_right)


def solution(mesh):
    in_specs = (
        P(("groups", "dp"), "tensor"),
        P(("groups", "dp"), "tensor"),
        P("dp", "tensor", None, None),
        P("dp", "tensor", None, None),
        P(None, "tensor"),
        P(None, "tensor"),
        P("tensor", None),
        P("tensor", None),
    )
    out_specs = (
        P(("groups", "dp"), "tensor"),
        P(("groups", "dp"), "tensor", None, None),
        P(("groups", "dp"), "tensor", None, None),
        P(("groups", "dp"), "tensor"),
        P(("groups", "dp"), "tensor"),
    )
    return jax.shard_map(shards, mesh=mesh, in_specs=in_specs, out_specs=out_specs, check_vma=False)
```

```python
import math

import jax
import jax.numpy as jnp
from jax import lax
from jax.sharding import PartitionSpec as P

root_coef = 0.7978845608028654
cubic_coef = 0.044715


def swapped(block, axis, distance):
    count = lax.axis_size(axis)
    route = []
    for low in range(count):
        high = low | 1 << distance
        if high != low and high < count:
            route += [(low, high), (high, low)]
    return lax.ppermute(block, axis, route)


def fetch_share(block):
    group_count = lax.axis_size("groups")
    rows = block.shape[0]
    if group_count == 1 or rows % group_count:
        return lax.all_gather(block, "dp", axis=0, tiled=True)
    share = rows // group_count
    mine = lax.dynamic_slice_in_dim(block, lax.axis_index("groups") * share, share, axis=0)
    return lax.all_gather(mine, "dp", axis=0, tiled=False)


def swap_shares(fetched, block):
    group_count = lax.axis_size("groups")
    if group_count == 1 or block.shape[0] % group_count:
        return fetched
    group = lax.axis_index("groups")
    received = [fetched] + [
        lax.ppermute(fetched, "groups", [(g, (g + shift) % group_count) for g in range(group_count)])
        for shift in range(1, group_count)
    ]
    reverse = jnp.stack(received[::-1], axis=1)
    doubled = jnp.concatenate([reverse, reverse], axis=1)
    ordered = lax.dynamic_slice_in_dim(doubled, group_count - 1 - group, group_count, axis=1)
    return ordered.reshape((-1,) + block.shape[1:])


def split_rows(values, axis, count):
    rows = values.shape[axis] // count
    return [lax.slice_in_dim(values, d * rows, (d + 1) * rows, axis=axis) for d in range(count)]


def butterfly_sum(values, axis):
    count = lax.axis_size(axis)
    if count & (count - 1):
        return lax.psum(values.astype(jnp.bfloat16), axis).astype(jnp.float32)
    total = values
    distance = 0
    while (1 << distance) < count:
        total = total + swapped(total, axis, distance)
        distance += 1
    return total


def gelu_pair(values):
    inner_arg = root_coef * (values + cubic_coef * values * values * values)
    tangent = jnp.tanh(inner_arg)
    forward = 0.5 * values * (1.0 + tangent)
    slopes = 0.5 * (1.0 + tangent) + 0.5 * values * (1.0 - tangent * tangent) * root_coef * (
        1.0 + 3.0 * cubic_coef * values * values
    )
    return (forward, slopes)


def pick_blocks(slices, pattern, block_size):
    picked = []
    for which_section, source in enumerate(slices):
        shaped = source.reshape(source.shape[0], -1, block_size)
        picked.append(jnp.take(shaped, pattern[:, which_section], axis=1))
    return jnp.stack(picked, axis=2)


def shards(
    inputs, cotangent, up_blocks, down_blocks, low_left, low_right, up_pattern, down_pattern
):
    tokens_here, width_here = inputs.shape
    block_size = up_blocks.shape[3]
    hidden_here = up_blocks.shape[1]
    section_count = up_blocks.shape[2]
    blocks_here = width_here // block_size
    dp_size = lax.axis_size("dp")
    inv_root = 1.0 / math.sqrt(tokens_here * dp_size)
    up_fetched = fetch_share(up_blocks)
    down_fetched = fetch_share(down_blocks)
    up_full = swap_shares(up_fetched, up_blocks)
    sources = [inputs] + [
        swapped(inputs, "tensor", level_bit) for level_bit in range(section_count - 1)
    ]
    selected = pick_blocks(sources, up_pattern, block_size)
    sparse = jnp.einsum("thsi,ihsj->thj", selected, up_full, preferred_element_type=jnp.float32)
    low_part = lax.dot_general(
        inputs, low_left, (((1,), (1,)), ((), ())), preferred_element_type=jnp.float32
    )
    low_sum = butterfly_sum(low_part, "tensor").astype(jnp.bfloat16)
    preact = sparse.reshape(tokens_here, -1) + jnp.dot(
        low_sum, low_right, preferred_element_type=jnp.float32
    )
    activated, slopes = gelu_pair(preact)
    hidden = activated.astype(jnp.bfloat16)
    picked = pick_blocks([cotangent] * section_count, down_pattern, block_size)
    hidden_blocks = hidden.reshape(tokens_here, hidden_here, block_size)
    down_parts = (
        jnp.stack(
            [
                jnp.einsum("thj,thso->hjso", rows, picked, preferred_element_type=jnp.float32)
                for rows in split_rows(hidden_blocks, 2, dp_size)
            ]
        )
        * inv_root
    ).astype(jnp.bfloat16)
    down_parts, down_fetched = lax.optimization_barrier((down_parts, down_fetched))
    down_full = swap_shares(down_fetched, down_blocks)
    grad_down = lax.psum_scatter(
        down_parts, "dp", scatter_dimension=0, tiled=False
    ).astype(jnp.float32)
    grad_down = jnp.transpose(grad_down, (1, 0, 2, 3))
    grad_hidden = jnp.einsum(
        "thso,jhso->thj", picked, down_full, preferred_element_type=jnp.float32
    ).reshape(tokens_here, -1)
    grad_pre = (grad_hidden * slopes).astype(jnp.bfloat16)
    grad_blocks = grad_pre.reshape(tokens_here, hidden_here, block_size)
    up_parts = jnp.stack(
        [
            jnp.einsum("thsi,thj->hsij", rows, grad_blocks, preferred_element_type=jnp.float32)
            for rows in split_rows(selected, 3, dp_size)
        ]
    )
    slot_ids = jnp.arange(blocks_here, dtype=jnp.int32)

    def section_term(which_section):
        spread = jnp.einsum(
            "thj,ihj->thi",
            grad_blocks,
            up_full[:, :, which_section, :],
            preferred_element_type=jnp.float32,
        )
        placing = (up_pattern[:, which_section][:, None] == slot_ids[None, :]).astype(jnp.float32)
        return jnp.einsum("thi,hd->tdi", spread, placing).reshape(tokens_here, width_here)

    own_term = section_term(0)
    for level_bit in range(section_count - 1):
        outgoing = section_term(level_bit + 1).astype(jnp.bfloat16)
        own_term = own_term + swapped(outgoing, "tensor", level_bit).astype(jnp.float32)
    back_part = lax.dot_general(
        grad_pre, low_right, (((1,), (1,)), ((), ())), preferred_element_type=jnp.float32
    )
    back_low = butterfly_sum(back_part, "tensor").astype(jnp.bfloat16)
    grad_input = (
        own_term + jnp.dot(back_low, low_left, preferred_element_type=jnp.float32)
    ).astype(jnp.bfloat16)
    up_parts, _ = lax.optimization_barrier(((up_parts * inv_root).astype(jnp.bfloat16), grad_down))
    grad_up = lax.psum_scatter(up_parts, "dp", scatter_dimension=0, tiled=False).astype(jnp.float32)
    row_part, low_row_part, grad_up = lax.optimization_barrier((back_low, low_sum, grad_up))
    grad_up = jnp.transpose(grad_up, (2, 0, 1, 3))
    grad_left = lax.psum_scatter(
        (
            lax.dot_general(
                row_part, inputs, (((0,), (0,)), ((), ())), preferred_element_type=jnp.float32
            )
            * inv_root
        ).astype(jnp.bfloat16),
        "dp",
        scatter_dimension=0,
        tiled=True,
    ).astype(jnp.float32)
    grad_right = lax.psum_scatter(
        (
            lax.dot_general(
                low_row_part, grad_pre, (((0,), (0,)), ((), ())), preferred_element_type=jnp.float32
            )
            * inv_root
        ).astype(jnp.bfloat16),
        "dp",
        scatter_dimension=0,
        tiled=True,
    ).astype(jnp.float32)
    return (grad_input, grad_up, grad_down, grad_left, grad_right)


def solution(mesh):
    in_specs = (
        P(("groups", "dp"), "tensor"),
        P(("groups", "dp"), "tensor"),
        P("dp", "tensor", None, None),
        P("dp", "tensor", None, None),
        P(None, "tensor"),
        P(None, "tensor"),
        P("tensor", None),
        P("tensor", None),
    )
    out_specs = (
        P(("groups", "dp"), "tensor"),
        P(("groups", "dp"), "tensor", None, None),
        P(("groups", "dp"), "tensor", None, None),
        P(("groups", "dp"), "tensor"),
        P(("groups", "dp"), "tensor"),
    )
    return jax.shard_map(shards, mesh=mesh, in_specs=in_specs, out_specs=out_specs, check_vma=False)
```

```python
import math

import jax
import jax.numpy as jnp
from jax import lax
from jax.sharding import PartitionSpec as P

root_coef = 0.7978845608028654
cubic_coef = 0.044715


def swapped(block, axis, distance):
    count = lax.axis_size(axis)
    route = []
    for low in range(count):
        high = low | 1 << distance
        if high != low and high < count:
            route += [(low, high), (high, low)]
    return lax.ppermute(block, axis, route)


def fetch_share(block):
    group_count = lax.axis_size("groups")
    rows = block.shape[0]
    if group_count == 1 or rows % group_count:
        return lax.all_gather(block, "dp", axis=0, tiled=True)
    share = rows // group_count
    mine = lax.dynamic_slice_in_dim(block, lax.axis_index("groups") * share, share, axis=0)
    return lax.all_gather(mine, "dp", axis=0, tiled=False)


def rotated(values, start):
    count = values.shape[0]
    doubled = jnp.concatenate([values, values], axis=0)
    return lax.dynamic_slice_in_dim(doubled, start % count, count, axis=0)


def swap_shares(fetched, block):
    group_count = lax.axis_size("groups")
    if group_count == 1 or block.shape[0] % group_count:
        return fetched
    group = lax.axis_index("groups")
    if group_count == 2:
        count = fetched.shape[0]
        me = lax.axis_index("dp")
        send = rotated(fetched, me + 1)[: count - 1]
        got = lax.ppermute(send, "groups", [(0, 1), (1, 0)])
        share = block.shape[0] // 2
        local = lax.dynamic_slice_in_dim(block, (1 - group) * share, share, axis=0)
        other = rotated(jnp.concatenate([got, local[None]], axis=0), count - 1 - me)
        received = [fetched, other]
    else:
        received = [fetched] + [
            lax.ppermute(
                fetched, "groups", [(g, (g + shift) % group_count) for g in range(group_count)]
            )
            for shift in range(1, group_count)
        ]
    reverse = jnp.stack(received[::-1], axis=1)
    doubled = jnp.concatenate([reverse, reverse], axis=1)
    ordered = lax.dynamic_slice_in_dim(doubled, group_count - 1 - group, group_count, axis=1)
    return ordered.reshape((-1,) + block.shape[1:])


def split_rows(values, axis, count):
    rows = values.shape[axis] // count
    return [lax.slice_in_dim(values, d * rows, (d + 1) * rows, axis=axis) for d in range(count)]


def butterfly_sum(values, axis):
    count = lax.axis_size(axis)
    if count & (count - 1):
        return lax.psum(values.astype(jnp.bfloat16), axis).astype(jnp.float32)
    total = values
    distance = 0
    while (1 << distance) < count:
        total = total + swapped(total, axis, distance)
        distance += 1
    return total


def gelu_pair(values):
    inner_arg = root_coef * (values + cubic_coef * values * values * values)
    tangent = jnp.tanh(inner_arg)
    forward = 0.5 * values * (1.0 + tangent)
    slopes = 0.5 * (1.0 + tangent) + 0.5 * values * (1.0 - tangent * tangent) * root_coef * (
        1.0 + 3.0 * cubic_coef * values * values
    )
    return (forward, slopes)


def pick_blocks(slices, pattern, block_size):
    picked = []
    for which_section, source in enumerate(slices):
        shaped = source.reshape(source.shape[0], -1, block_size)
        picked.append(jnp.take(shaped, pattern[:, which_section], axis=1))
    return jnp.stack(picked, axis=2)


def shards(
    inputs, cotangent, up_blocks, down_blocks, low_left, low_right, up_pattern, down_pattern
):
    tokens_here, width_here = inputs.shape
    block_size = up_blocks.shape[3]
    hidden_here = up_blocks.shape[1]
    section_count = up_blocks.shape[2]
    blocks_here = width_here // block_size
    dp_size = lax.axis_size("dp")
    inv_root = 1.0 / math.sqrt(tokens_here * dp_size)
    up_fetched = fetch_share(up_blocks)
    down_fetched = fetch_share(down_blocks)
    up_full = swap_shares(up_fetched, up_blocks)
    sources = [inputs] + [
        swapped(inputs, "tensor", level_bit) for level_bit in range(section_count - 1)
    ]
    selected = pick_blocks(sources, up_pattern, block_size)
    sparse = jnp.einsum("thsi,ihsj->thj", selected, up_full, preferred_element_type=jnp.float32)
    low_part = lax.dot_general(
        inputs, low_left, (((1,), (1,)), ((), ())), preferred_element_type=jnp.float32
    )
    low_sum = butterfly_sum(low_part, "tensor").astype(jnp.bfloat16)
    preact = sparse.reshape(tokens_here, -1) + jnp.dot(
        low_sum, low_right, preferred_element_type=jnp.float32
    )
    activated, slopes = gelu_pair(preact)
    hidden = activated.astype(jnp.bfloat16)
    picked = pick_blocks([cotangent] * section_count, down_pattern, block_size)
    hidden_blocks = hidden.reshape(tokens_here, hidden_here, block_size)
    down_parts = (
        jnp.stack(
            [
                jnp.einsum("thj,thso->hjso", rows, picked, preferred_element_type=jnp.float32)
                for rows in split_rows(hidden_blocks, 2, dp_size)
            ]
        )
        * inv_root
    ).astype(jnp.bfloat16)
    down_parts, down_fetched = lax.optimization_barrier((down_parts, down_fetched))
    down_full = swap_shares(down_fetched, down_blocks)
    grad_down = lax.psum_scatter(
        down_parts, "dp", scatter_dimension=0, tiled=False
    ).astype(jnp.float32)
    grad_down = jnp.transpose(grad_down, (1, 0, 2, 3))
    grad_hidden = jnp.einsum(
        "thso,jhso->thj", picked, down_full, preferred_element_type=jnp.float32
    ).reshape(tokens_here, -1)
    grad_pre = (grad_hidden * slopes).astype(jnp.bfloat16)
    grad_blocks = grad_pre.reshape(tokens_here, hidden_here, block_size)
    up_parts = jnp.stack(
        [
            jnp.einsum("thsi,thj->hsij", rows, grad_blocks, preferred_element_type=jnp.float32)
            for rows in split_rows(selected, 3, dp_size)
        ]
    )
    slot_ids = jnp.arange(blocks_here, dtype=jnp.int32)

    def section_term(which_section):
        spread = jnp.einsum(
            "thj,ihj->thi",
            grad_blocks,
            up_full[:, :, which_section, :],
            preferred_element_type=jnp.float32,
        )
        placing = (up_pattern[:, which_section][:, None] == slot_ids[None, :]).astype(jnp.float32)
        return jnp.einsum("thi,hd->tdi", spread, placing).reshape(tokens_here, width_here)

    own_term = section_term(0)
    for level_bit in range(section_count - 1):
        outgoing = section_term(level_bit + 1).astype(jnp.bfloat16)
        own_term = own_term + swapped(outgoing, "tensor", level_bit).astype(jnp.float32)
    back_part = lax.dot_general(
        grad_pre, low_right, (((1,), (1,)), ((), ())), preferred_element_type=jnp.float32
    )
    back_low = butterfly_sum(back_part, "tensor").astype(jnp.bfloat16)
    grad_input = (
        own_term + jnp.dot(back_low, low_left, preferred_element_type=jnp.float32)
    ).astype(jnp.bfloat16)
    up_parts, _ = lax.optimization_barrier(((up_parts * inv_root).astype(jnp.bfloat16), grad_down))
    grad_up = lax.psum_scatter(up_parts, "dp", scatter_dimension=0, tiled=False).astype(jnp.float32)
    row_part, low_row_part, grad_up = lax.optimization_barrier((back_low, low_sum, grad_up))
    grad_up = jnp.transpose(grad_up, (2, 0, 1, 3))
    grad_left = lax.psum_scatter(
        (
            lax.dot_general(
                row_part, inputs, (((0,), (0,)), ((), ())), preferred_element_type=jnp.float32
            )
            * inv_root
        ).astype(jnp.bfloat16),
        "dp",
        scatter_dimension=0,
        tiled=True,
    ).astype(jnp.float32)
    grad_right = lax.psum_scatter(
        (
            lax.dot_general(
                low_row_part, grad_pre, (((0,), (0,)), ((), ())), preferred_element_type=jnp.float32
            )
            * inv_root
        ).astype(jnp.bfloat16),
        "dp",
        scatter_dimension=0,
        tiled=True,
    ).astype(jnp.float32)
    return (grad_input, grad_up, grad_down, grad_left, grad_right)


def solution(mesh):
    in_specs = (
        P(("groups", "dp"), "tensor"),
        P(("groups", "dp"), "tensor"),
        P("dp", "tensor", None, None),
        P("dp", "tensor", None, None),
        P(None, "tensor"),
        P(None, "tensor"),
        P("tensor", None),
        P("tensor", None),
    )
    out_specs = (
        P(("groups", "dp"), "tensor"),
        P(("groups", "dp"), "tensor", None, None),
        P(("groups", "dp"), "tensor", None, None),
        P(("groups", "dp"), "tensor"),
        P(("groups", "dp"), "tensor"),
    )
    return jax.shard_map(shards, mesh=mesh, in_specs=in_specs, out_specs=out_specs, check_vma=False)
```

```python
import math

import jax
import jax.numpy as jnp
from jax import lax
from jax.sharding import PartitionSpec as P

root_coef = 0.7978845608028654
cubic_coef = 0.044715


def swapped(block, axis, distance):
    count = lax.axis_size(axis)
    route = []
    for low in range(count):
        high = low | 1 << distance
        if high != low and high < count:
            route += [(low, high), (high, low)]
    return lax.ppermute(block, axis, route)


def fetch_share(block):
    group_count = lax.axis_size("groups")
    rows = block.shape[0]
    if group_count == 1 or rows % group_count:
        return lax.all_gather(block, "dp", axis=0, tiled=True)
    share = rows // group_count
    mine = lax.dynamic_slice_in_dim(block, lax.axis_index("groups") * share, share, axis=0)
    return lax.all_gather(mine, "dp", axis=0, tiled=False)


def rotated(values, start):
    count = values.shape[0]
    doubled = jnp.concatenate([values, values], axis=0)
    return lax.dynamic_slice_in_dim(doubled, start % count, count, axis=0)


def swap_shares(fetched, block):
    group_count = lax.axis_size("groups")
    if group_count == 1 or block.shape[0] % group_count:
        return fetched
    group = lax.axis_index("groups")
    if group_count == 2:
        count = fetched.shape[0]
        me = lax.axis_index("dp")
        send = rotated(fetched, me + 1)[: count - 1]
        got = lax.ppermute(send, "groups", [(0, 1), (1, 0)])
        share = block.shape[0] // 2
        local = lax.dynamic_slice_in_dim(block, (1 - group) * share, share, axis=0)
        other = rotated(jnp.concatenate([got, local[None]], axis=0), count - 1 - me)
        received = [fetched, other]
    else:
        received = [fetched] + [
            lax.ppermute(
                fetched, "groups", [(g, (g + shift) % group_count) for g in range(group_count)]
            )
            for shift in range(1, group_count)
        ]
    reverse = jnp.stack(received[::-1], axis=1)
    doubled = jnp.concatenate([reverse, reverse], axis=1)
    ordered = lax.dynamic_slice_in_dim(doubled, group_count - 1 - group, group_count, axis=1)
    return ordered.reshape((-1,) + block.shape[1:])


def split_rows(values, axis, count):
    rows = values.shape[axis] // count
    return [lax.slice_in_dim(values, d * rows, (d + 1) * rows, axis=axis) for d in range(count)]


def butterfly_sum(values, axis):
    count = lax.axis_size(axis)
    if count & (count - 1):
        return lax.psum(values.astype(jnp.bfloat16), axis).astype(jnp.float32)
    total = values
    distance = 0
    while (1 << distance) < count:
        total = total + swapped(total, axis, distance)
        distance += 1
    return total


def gelu_pair(values):
    inner_arg = root_coef * (values + cubic_coef * values * values * values)
    tangent = jnp.tanh(inner_arg)
    forward = 0.5 * values * (1.0 + tangent)
    slopes = 0.5 * (1.0 + tangent) + 0.5 * values * (1.0 - tangent * tangent) * root_coef * (
        1.0 + 3.0 * cubic_coef * values * values
    )
    return (forward, slopes)


def pick_blocks(slices, pattern, block_size):
    picked = []
    for which_section, source in enumerate(slices):
        shaped = source.reshape(source.shape[0], -1, block_size)
        picked.append(jnp.take(shaped, pattern[:, which_section], axis=1))
    return jnp.stack(picked, axis=2)


def shards(
    inputs, cotangent, up_blocks, down_blocks, low_left, low_right, up_pattern, down_pattern
):
    tokens_here, width_here = inputs.shape
    block_size = up_blocks.shape[3]
    hidden_here = up_blocks.shape[1]
    section_count = up_blocks.shape[2]
    blocks_here = width_here // block_size
    dp_size = lax.axis_size("dp")
    inv_root = 1.0 / math.sqrt(tokens_here * dp_size)
    up_fetched = fetch_share(up_blocks)
    down_fetched = fetch_share(down_blocks)
    up_full = swap_shares(up_fetched, up_blocks)
    sources = [inputs] + [
        swapped(inputs, "tensor", level_bit) for level_bit in range(section_count - 1)
    ]
    selected = pick_blocks(sources, up_pattern, block_size)
    sparse = jnp.einsum("thsi,ihsj->thj", selected, up_full, preferred_element_type=jnp.float32)
    low_part = lax.dot_general(
        inputs, low_left, (((1,), (1,)), ((), ())), preferred_element_type=jnp.float32
    )
    low_sum = butterfly_sum(low_part, "tensor").astype(jnp.bfloat16)
    preact = sparse.reshape(tokens_here, -1) + jnp.dot(
        low_sum, low_right, preferred_element_type=jnp.float32
    )
    activated, slopes = gelu_pair(preact)
    hidden = activated.astype(jnp.bfloat16)
    picked = pick_blocks([cotangent] * section_count, down_pattern, block_size)
    hidden_blocks = hidden.reshape(tokens_here, hidden_here, block_size)
    down_parts = (
        jnp.stack(
            [
                jnp.einsum("thj,thso->hjso", rows, picked, preferred_element_type=jnp.float32)
                for rows in split_rows(hidden_blocks, 2, dp_size)
            ]
        )
        * inv_root
    ).astype(jnp.bfloat16)
    down_parts, down_fetched = lax.optimization_barrier((down_parts, down_fetched))
    down_full = swap_shares(down_fetched, down_blocks)
    grad_down = lax.psum_scatter(
        down_parts, "dp", scatter_dimension=0, tiled=False
    ).astype(jnp.float32)
    grad_down = jnp.transpose(grad_down, (1, 0, 2, 3))
    grad_hidden = jnp.einsum(
        "thso,jhso->thj", picked, down_full, preferred_element_type=jnp.float32
    ).reshape(tokens_here, -1)
    grad_pre = (grad_hidden * slopes).astype(jnp.bfloat16)
    grad_blocks = grad_pre.reshape(tokens_here, hidden_here, block_size)
    up_parts = jnp.stack(
        [
            jnp.einsum("thsi,thj->hsij", rows, grad_blocks, preferred_element_type=jnp.float32)
            for rows in split_rows(selected, 3, dp_size)
        ]
    )
    slot_ids = jnp.arange(blocks_here, dtype=jnp.int32)

    def section_term(which_section):
        spread = jnp.einsum(
            "thj,ihj->thi",
            grad_blocks,
            up_full[:, :, which_section, :],
            preferred_element_type=jnp.float32,
        )
        placing = (up_pattern[:, which_section][:, None] == slot_ids[None, :]).astype(jnp.float32)
        return jnp.einsum("thi,hd->tdi", spread, placing).reshape(tokens_here, width_here)

    incoming = [
        swapped(section_term(level_bit + 1).astype(jnp.bfloat16), "tensor", level_bit)
        for level_bit in range(section_count - 1)
    ]
    up_parts, incoming, _ = lax.optimization_barrier(
        ((up_parts * inv_root).astype(jnp.bfloat16), incoming, grad_down)
    )
    own_term = section_term(0)
    for level_bit in range(section_count - 1):
        own_term = own_term + incoming[level_bit].astype(jnp.float32)
    back_part = lax.dot_general(
        grad_pre, low_right, (((1,), (1,)), ((), ())), preferred_element_type=jnp.float32
    )
    back_low = butterfly_sum(back_part, "tensor").astype(jnp.bfloat16)
    grad_input = (
        own_term + jnp.dot(back_low, low_left, preferred_element_type=jnp.float32)
    ).astype(jnp.bfloat16)
    grad_up = lax.psum_scatter(up_parts, "dp", scatter_dimension=0, tiled=False).astype(jnp.float32)
    row_part, low_row_part, grad_up = lax.optimization_barrier((back_low, low_sum, grad_up))
    grad_up = jnp.transpose(grad_up, (2, 0, 1, 3))
    left_parts = jnp.stack(
        split_rows(
            lax.dot_general(
                row_part, inputs, (((0,), (0,)), ((), ())), preferred_element_type=jnp.float32
            ),
            0,
            dp_size,
        )
    )
    right_parts = jnp.stack(
        split_rows(
            lax.dot_general(
                low_row_part, grad_pre, (((0,), (0,)), ((), ())), preferred_element_type=jnp.float32
            ),
            0,
            dp_size,
        )
    )
    joined = (jnp.concatenate([left_parts, right_parts], axis=2) * inv_root).astype(jnp.bfloat16)
    joined = lax.psum_scatter(joined, "dp", scatter_dimension=0, tiled=False).astype(jnp.float32)
    grad_left = joined[:, :width_here]
    grad_right = joined[:, width_here:]
    return (grad_input, grad_up, grad_down, grad_left, grad_right)


def solution(mesh):
    in_specs = (
        P(("groups", "dp"), "tensor"),
        P(("groups", "dp"), "tensor"),
        P("dp", "tensor", None, None),
        P("dp", "tensor", None, None),
        P(None, "tensor"),
        P(None, "tensor"),
        P("tensor", None),
        P("tensor", None),
    )
    out_specs = (
        P(("groups", "dp"), "tensor"),
        P(("groups", "dp"), "tensor", None, None),
        P(("groups", "dp"), "tensor", None, None),
        P(("groups", "dp"), "tensor"),
        P(("groups", "dp"), "tensor"),
    )
    return jax.shard_map(shards, mesh=mesh, in_specs=in_specs, out_specs=out_specs, check_vma=False)
```

```python
import math

import jax
import jax.numpy as jnp
from jax import lax
from jax.sharding import PartitionSpec as P

root_coef = 0.7978845608028654
cubic_coef = 0.044715


def swapped(block, axis, distance):
    count = lax.axis_size(axis)
    route = []
    for low in range(count):
        high = low | 1 << distance
        if high != low and high < count:
            route += [(low, high), (high, low)]
    return lax.ppermute(block, axis, route)


def fetch_share(block):
    group_count = lax.axis_size("groups")
    rows = block.shape[0]
    if group_count == 1 or rows % group_count:
        return lax.all_gather(block, "dp", axis=0, tiled=True)
    share = rows // group_count
    mine = lax.dynamic_slice_in_dim(block, lax.axis_index("groups") * share, share, axis=0)
    return lax.all_gather(mine, "dp", axis=0, tiled=False)


def rotated(values, start):
    count = values.shape[0]
    doubled = jnp.concatenate([values, values], axis=0)
    return lax.dynamic_slice_in_dim(doubled, start % count, count, axis=0)


def swap_shares(fetched, block):
    group_count = lax.axis_size("groups")
    if group_count == 1 or block.shape[0] % group_count:
        return fetched
    group = lax.axis_index("groups")
    if group_count == 2:
        count = fetched.shape[0]
        me = lax.axis_index("dp")
        send = rotated(fetched, me + 1)[: count - 1]
        got = lax.ppermute(send, "groups", [(0, 1), (1, 0)])
        share = block.shape[0] // 2
        local = lax.dynamic_slice_in_dim(block, (1 - group) * share, share, axis=0)
        other = rotated(jnp.concatenate([got, local[None]], axis=0), count - 1 - me)
        received = [fetched, other]
    else:
        received = [fetched] + [
            lax.ppermute(
                fetched, "groups", [(g, (g + shift) % group_count) for g in range(group_count)]
            )
            for shift in range(1, group_count)
        ]
    reverse = jnp.stack(received[::-1], axis=1)
    doubled = jnp.concatenate([reverse, reverse], axis=1)
    ordered = lax.dynamic_slice_in_dim(doubled, group_count - 1 - group, group_count, axis=1)
    return ordered.reshape((-1,) + block.shape[1:])


def split_rows(values, axis, count):
    rows = values.shape[axis] // count
    return [lax.slice_in_dim(values, d * rows, (d + 1) * rows, axis=axis) for d in range(count)]


def butterfly_sum(values, axis):
    count = lax.axis_size(axis)
    if count & (count - 1):
        return lax.psum(values.astype(jnp.bfloat16), axis).astype(jnp.float32)
    total = values
    distance = 0
    while (1 << distance) < count:
        total = total + swapped(total, axis, distance)
        distance += 1
    return total


def gelu_pair(values):
    inner_arg = root_coef * (values + cubic_coef * values * values * values)
    tangent = jnp.tanh(inner_arg)
    forward = 0.5 * values * (1.0 + tangent)
    slopes = 0.5 * (1.0 + tangent) + 0.5 * values * (1.0 - tangent * tangent) * root_coef * (
        1.0 + 3.0 * cubic_coef * values * values
    )
    return (forward, slopes)


def pick_blocks(slices, pattern, block_size):
    picked = []
    for which_section, source in enumerate(slices):
        shaped = source.reshape(source.shape[0], -1, block_size)
        picked.append(jnp.take(shaped, pattern[:, which_section], axis=1))
    return jnp.stack(picked, axis=2)


def shards(
    inputs, cotangent, up_blocks, down_blocks, low_left, low_right, up_pattern, down_pattern
):
    tokens_here, width_here = inputs.shape
    block_size = up_blocks.shape[3]
    hidden_here = up_blocks.shape[1]
    section_count = up_blocks.shape[2]
    blocks_here = width_here // block_size
    dp_size = lax.axis_size("dp")
    inv_root = 1.0 / math.sqrt(tokens_here * dp_size)
    up_fetched = fetch_share(up_blocks)
    down_fetched = fetch_share(down_blocks)
    up_full = swap_shares(up_fetched, up_blocks)
    sources = [inputs] + [
        swapped(inputs, "tensor", level_bit) for level_bit in range(section_count - 1)
    ]
    selected = pick_blocks(sources, up_pattern, block_size)
    sparse = jnp.einsum("thsi,ihsj->thj", selected, up_full, preferred_element_type=jnp.float32)
    low_part = lax.dot_general(
        inputs, low_left, (((1,), (1,)), ((), ())), preferred_element_type=jnp.float32
    )
    low_sum = butterfly_sum(low_part, "tensor").astype(jnp.bfloat16)
    preact = sparse.reshape(tokens_here, -1) + jnp.dot(
        low_sum, low_right, preferred_element_type=jnp.float32
    )
    activated, slopes = gelu_pair(preact)
    hidden = activated.astype(jnp.bfloat16)
    picked = pick_blocks([cotangent] * section_count, down_pattern, block_size)
    hidden_blocks = hidden.reshape(tokens_here, hidden_here, block_size)
    down_parts = (
        jnp.stack(
            [
                jnp.einsum("thj,thso->hjso", rows, picked, preferred_element_type=jnp.float32)
                for rows in split_rows(hidden_blocks, 2, dp_size)
            ]
        )
        * inv_root
    ).astype(jnp.bfloat16)
    down_parts, down_fetched = lax.optimization_barrier((down_parts, down_fetched))
    down_full = swap_shares(down_fetched, down_blocks)
    down_summed = lax.psum_scatter(down_parts, "dp", scatter_dimension=0, tiled=False)
    grad_hidden = jnp.einsum(
        "thso,jhso->thj", picked, down_full, preferred_element_type=jnp.float32
    ).reshape(tokens_here, -1)
    grad_pre = (grad_hidden * slopes).astype(jnp.bfloat16)
    grad_blocks = grad_pre.reshape(tokens_here, hidden_here, block_size)
    up_parts = jnp.stack(
        [
            jnp.einsum("thsi,thj->hsij", rows, grad_blocks, preferred_element_type=jnp.float32)
            for rows in split_rows(selected, 3, dp_size)
        ]
    )
    slot_ids = jnp.arange(blocks_here, dtype=jnp.int32)

    def section_term(which_section):
        spread = jnp.einsum(
            "thj,ihj->thi",
            grad_blocks,
            up_full[:, :, which_section, :],
            preferred_element_type=jnp.float32,
        )
        placing = (up_pattern[:, which_section][:, None] == slot_ids[None, :]).astype(jnp.float32)
        return jnp.einsum("thi,hd->tdi", spread, placing).reshape(tokens_here, width_here)

    incoming = [
        swapped(section_term(level_bit + 1).astype(jnp.bfloat16), "tensor", level_bit)
        for level_bit in range(section_count - 1)
    ]
    up_parts, down_summed = lax.optimization_barrier(
        ((up_parts * inv_root).astype(jnp.bfloat16), down_summed)
    )
    grad_down = jnp.transpose(down_summed.astype(jnp.float32), (1, 0, 2, 3))
    back_part = lax.dot_general(
        grad_pre, low_right, (((1,), (1,)), ((), ())), preferred_element_type=jnp.float32
    )
    back_low = butterfly_sum(back_part, "tensor").astype(jnp.bfloat16)
    grad_up = lax.psum_scatter(up_parts, "dp", scatter_dimension=0, tiled=False).astype(jnp.float32)
    row_part, low_row_part, grad_up, incoming = lax.optimization_barrier(
        (back_low, low_sum, grad_up, incoming)
    )
    own_term = section_term(0)
    for level_bit in range(section_count - 1):
        own_term = own_term + incoming[level_bit].astype(jnp.float32)
    grad_input = (
        own_term + jnp.dot(back_low, low_left, preferred_element_type=jnp.float32)
    ).astype(jnp.bfloat16)
    grad_up = jnp.transpose(grad_up, (2, 0, 1, 3))
    left_parts = jnp.stack(
        split_rows(
            lax.dot_general(
                row_part, inputs, (((0,), (0,)), ((), ())), preferred_element_type=jnp.float32
            ),
            0,
            dp_size,
        )
    )
    right_parts = jnp.stack(
        split_rows(
            lax.dot_general(
                low_row_part, grad_pre, (((0,), (0,)), ((), ())), preferred_element_type=jnp.float32
            ),
            0,
            dp_size,
        )
    )
    joined = (jnp.concatenate([left_parts, right_parts], axis=2) * inv_root).astype(jnp.bfloat16)
    joined = lax.psum_scatter(joined, "dp", scatter_dimension=0, tiled=False).astype(jnp.float32)
    grad_left = joined[:, :width_here]
    grad_right = joined[:, width_here:]
    return (grad_input, grad_up, grad_down, grad_left, grad_right)


def solution(mesh):
    in_specs = (
        P(("groups", "dp"), "tensor"),
        P(("groups", "dp"), "tensor"),
        P("dp", "tensor", None, None),
        P("dp", "tensor", None, None),
        P(None, "tensor"),
        P(None, "tensor"),
        P("tensor", None),
        P("tensor", None),
    )
    out_specs = (
        P(("groups", "dp"), "tensor"),
        P(("groups", "dp"), "tensor", None, None),
        P(("groups", "dp"), "tensor", None, None),
        P(("groups", "dp"), "tensor"),
        P(("groups", "dp"), "tensor"),
    )
    return jax.shard_map(shards, mesh=mesh, in_specs=in_specs, out_specs=out_specs, check_vma=False)
```

```python
import math

import jax
import jax.numpy as jnp
from jax import lax
from jax.sharding import PartitionSpec as P

root_coef = 0.7978845608028654
cubic_coef = 0.044715


def swapped(block, axis, distance):
    count = lax.axis_size(axis)
    route = []
    for low in range(count):
        high = low | 1 << distance
        if high != low and high < count:
            route += [(low, high), (high, low)]
    return lax.ppermute(block, axis, route)


def fetch_share(block):
    group_count = lax.axis_size("groups")
    rows = block.shape[0]
    if group_count == 1 or rows % group_count:
        return lax.all_gather(block, "dp", axis=0, tiled=True)
    share = rows // group_count
    mine = lax.dynamic_slice_in_dim(block, lax.axis_index("groups") * share, share, axis=0)
    return lax.all_gather(mine, "dp", axis=0, tiled=False)


def rotated(values, start):
    count = values.shape[0]
    doubled = jnp.concatenate([values, values], axis=0)
    return lax.dynamic_slice_in_dim(doubled, start % count, count, axis=0)


def swap_shares(fetched, block):
    group_count = lax.axis_size("groups")
    if group_count == 1 or block.shape[0] % group_count:
        return fetched
    group = lax.axis_index("groups")
    if group_count == 2:
        count = fetched.shape[0]
        me = lax.axis_index("dp")
        send = rotated(fetched, me + 1)[: count - 1]
        got = lax.ppermute(send, "groups", [(0, 1), (1, 0)])
        share = block.shape[0] // 2
        local = lax.dynamic_slice_in_dim(block, (1 - group) * share, share, axis=0)
        other = rotated(jnp.concatenate([got, local[None]], axis=0), count - 1 - me)
        received = [fetched, other]
    else:
        received = [fetched] + [
            lax.ppermute(
                fetched, "groups", [(g, (g + shift) % group_count) for g in range(group_count)]
            )
            for shift in range(1, group_count)
        ]
    reverse = jnp.stack(received[::-1], axis=1)
    doubled = jnp.concatenate([reverse, reverse], axis=1)
    ordered = lax.dynamic_slice_in_dim(doubled, group_count - 1 - group, group_count, axis=1)
    return ordered.reshape((-1,) + block.shape[1:])


def split_rows(values, axis, count):
    rows = values.shape[axis] // count
    return [lax.slice_in_dim(values, d * rows, (d + 1) * rows, axis=axis) for d in range(count)]


def butterfly_sum(values, axis):
    count = lax.axis_size(axis)
    if count & (count - 1):
        return lax.psum(values.astype(jnp.bfloat16), axis).astype(jnp.float32)
    total = values
    distance = 0
    while (1 << distance) < count:
        total = total + swapped(total, axis, distance)
        distance += 1
    return total


def gelu_pair(values):
    inner_arg = root_coef * (values + cubic_coef * values * values * values)
    tangent = jnp.tanh(inner_arg)
    forward = 0.5 * values * (1.0 + tangent)
    slopes = 0.5 * (1.0 + tangent) + 0.5 * values * (1.0 - tangent * tangent) * root_coef * (
        1.0 + 3.0 * cubic_coef * values * values
    )
    return (forward, slopes)


def pick_blocks(slices, pattern, block_size):
    picked = []
    for which_section, source in enumerate(slices):
        shaped = source.reshape(source.shape[0], -1, block_size)
        picked.append(jnp.take(shaped, pattern[:, which_section], axis=1))
    return jnp.stack(picked, axis=2)


def shards(
    inputs, cotangent, up_blocks, down_blocks, low_left, low_right, up_pattern, down_pattern
):
    tokens_here, width_here = inputs.shape
    block_size = up_blocks.shape[3]
    hidden_here = up_blocks.shape[1]
    section_count = up_blocks.shape[2]
    blocks_here = width_here // block_size
    dp_size = lax.axis_size("dp")
    inv_root = 1.0 / math.sqrt(tokens_here * dp_size)
    up_fetched = fetch_share(up_blocks)
    down_fetched = fetch_share(down_blocks)
    up_full = swap_shares(up_fetched, up_blocks)
    sources = [inputs] + [
        swapped(inputs, "tensor", level_bit) for level_bit in range(section_count - 1)
    ]
    selected = pick_blocks(sources, up_pattern, block_size)
    sparse = jnp.einsum("thsi,ihsj->htj", selected, up_full, preferred_element_type=jnp.float32)
    right_blocks = low_right.reshape(low_right.shape[0], hidden_here, block_size)
    low_part = lax.dot_general(
        inputs, low_left, (((1,), (1,)), ((), ())), preferred_element_type=jnp.float32
    )
    low_sum = butterfly_sum(low_part, "tensor").astype(jnp.bfloat16)
    preact = sparse + jnp.einsum(
        "tr,rhj->htj", low_sum, right_blocks, preferred_element_type=jnp.float32
    )
    activated, slopes = gelu_pair(preact)
    hidden = activated.astype(jnp.bfloat16)
    picked = pick_blocks([cotangent] * section_count, down_pattern, block_size)
    down_parts = (
        jnp.stack(
            [
                jnp.einsum("htj,thso->hjso", rows, picked, preferred_element_type=jnp.float32)
                for rows in split_rows(hidden, 2, dp_size)
            ]
        )
        * inv_root
    ).astype(jnp.bfloat16)
    down_parts, down_fetched = lax.optimization_barrier((down_parts, down_fetched))
    down_full = swap_shares(down_fetched, down_blocks)
    down_summed = lax.psum_scatter(down_parts, "dp", scatter_dimension=0, tiled=False)
    grad_hidden = jnp.einsum(
        "thso,jhso->htj", picked, down_full, preferred_element_type=jnp.float32
    )
    grad_blocks = (grad_hidden * slopes).astype(jnp.bfloat16)
    up_parts = jnp.stack(
        [
            jnp.einsum("thsi,htj->hsij", rows, grad_blocks, preferred_element_type=jnp.float32)
            for rows in split_rows(selected, 3, dp_size)
        ]
    )
    slot_ids = jnp.arange(blocks_here, dtype=jnp.int32)

    def section_term(which_section):
        spread = jnp.einsum(
            "htj,ihj->thi",
            grad_blocks,
            up_full[:, :, which_section, :],
            preferred_element_type=jnp.float32,
        )
        placing = (up_pattern[:, which_section][:, None] == slot_ids[None, :]).astype(jnp.float32)
        return jnp.einsum("thi,hd->tdi", spread, placing).reshape(tokens_here, width_here)

    incoming = [
        swapped(section_term(level_bit + 1).astype(jnp.bfloat16), "tensor", level_bit)
        for level_bit in range(section_count - 1)
    ]
    up_parts, down_summed = lax.optimization_barrier(
        ((up_parts * inv_root).astype(jnp.bfloat16), down_summed)
    )
    grad_down = jnp.transpose(down_summed.astype(jnp.float32), (1, 0, 2, 3))
    back_part = jnp.einsum(
        "htj,rhj->tr", grad_blocks, right_blocks, preferred_element_type=jnp.float32
    )
    back_low = butterfly_sum(back_part, "tensor").astype(jnp.bfloat16)
    grad_up = lax.psum_scatter(up_parts, "dp", scatter_dimension=0, tiled=False).astype(jnp.float32)
    row_part, low_row_part, grad_up, incoming = lax.optimization_barrier(
        (back_low, low_sum, grad_up, incoming)
    )
    own_term = section_term(0)
    for level_bit in range(section_count - 1):
        own_term = own_term + incoming[level_bit].astype(jnp.float32)
    grad_input = (
        own_term + jnp.dot(back_low, low_left, preferred_element_type=jnp.float32)
    ).astype(jnp.bfloat16)
    grad_up = jnp.transpose(grad_up, (2, 0, 1, 3))
    left_parts = jnp.stack(
        split_rows(
            lax.dot_general(
                row_part, inputs, (((0,), (0,)), ((), ())), preferred_element_type=jnp.float32
            ),
            0,
            dp_size,
        )
    )
    right_parts = jnp.stack(
        split_rows(
            jnp.einsum(
                "tr,htj->rhj", low_row_part, grad_blocks, preferred_element_type=jnp.float32
            ).reshape(low_row_part.shape[1], -1),
            0,
            dp_size,
        )
    )
    joined = (jnp.concatenate([left_parts, right_parts], axis=2) * inv_root).astype(jnp.bfloat16)
    joined = lax.psum_scatter(joined, "dp", scatter_dimension=0, tiled=False).astype(jnp.float32)
    grad_left = joined[:, :width_here]
    grad_right = joined[:, width_here:]
    return (grad_input, grad_up, grad_down, grad_left, grad_right)


def solution(mesh):
    in_specs = (
        P(("groups", "dp"), "tensor"),
        P(("groups", "dp"), "tensor"),
        P("dp", "tensor", None, None),
        P("dp", "tensor", None, None),
        P(None, "tensor"),
        P(None, "tensor"),
        P("tensor", None),
        P("tensor", None),
    )
    out_specs = (
        P(("groups", "dp"), "tensor"),
        P(("groups", "dp"), "tensor", None, None),
        P(("groups", "dp"), "tensor", None, None),
        P(("groups", "dp"), "tensor"),
        P(("groups", "dp"), "tensor"),
    )
    return jax.shard_map(shards, mesh=mesh, in_specs=in_specs, out_specs=out_specs, check_vma=False)
```

```python
import math

import jax
import jax.numpy as jnp
from jax import lax
from jax.sharding import PartitionSpec as P

root_coef = 0.7978845608028654
cubic_coef = 0.044715


def swapped(block, axis, distance):
    count = lax.axis_size(axis)
    route = []
    for low in range(count):
        high = low | 1 << distance
        if high != low and high < count:
            route += [(low, high), (high, low)]
    return lax.ppermute(block, axis, route)


def fetch_share(block):
    group_count = lax.axis_size("groups")
    rows = block.shape[0]
    if group_count == 1 or rows % group_count:
        return lax.all_gather(block, "dp", axis=0, tiled=True)
    share = rows // group_count
    mine = lax.dynamic_slice_in_dim(block, lax.axis_index("groups") * share, share, axis=0)
    return lax.all_gather(mine, "dp", axis=0, tiled=False)


def rotated(values, start):
    count = values.shape[0]
    doubled = jnp.concatenate([values, values], axis=0)
    return lax.dynamic_slice_in_dim(doubled, start % count, count, axis=0)


def swap_shares(fetched, block):
    group_count = lax.axis_size("groups")
    if group_count == 1 or block.shape[0] % group_count:
        return fetched
    group = lax.axis_index("groups")
    if group_count == 2:
        count = fetched.shape[0]
        me = lax.axis_index("dp")
        send = rotated(fetched, me + 1)[: count - 1]
        got = lax.ppermute(send, "groups", [(0, 1), (1, 0)])
        share = block.shape[0] // 2
        local = lax.dynamic_slice_in_dim(block, (1 - group) * share, share, axis=0)
        other = rotated(jnp.concatenate([got, local[None]], axis=0), count - 1 - me)
        received = [fetched, other]
    else:
        received = [fetched] + [
            lax.ppermute(
                fetched, "groups", [(g, (g + shift) % group_count) for g in range(group_count)]
            )
            for shift in range(1, group_count)
        ]
    reverse = jnp.stack(received[::-1], axis=1)
    doubled = jnp.concatenate([reverse, reverse], axis=1)
    ordered = lax.dynamic_slice_in_dim(doubled, group_count - 1 - group, group_count, axis=1)
    return ordered.reshape((-1,) + block.shape[1:])


def split_rows(values, axis, count):
    rows = values.shape[axis] // count
    return [lax.slice_in_dim(values, d * rows, (d + 1) * rows, axis=axis) for d in range(count)]


def butterfly_sum(values, axis):
    count = lax.axis_size(axis)
    if count & (count - 1):
        return lax.psum(values.astype(jnp.bfloat16), axis).astype(jnp.float32)
    total = values
    distance = 0
    while (1 << distance) < count:
        total = total + swapped(total, axis, distance)
        distance += 1
    return total


def gelu_pair(values):
    inner_arg = root_coef * (values + cubic_coef * values * values * values)
    tangent = jnp.tanh(inner_arg)
    forward = 0.5 * values * (1.0 + tangent)
    slopes = 0.5 * (1.0 + tangent) + 0.5 * values * (1.0 - tangent * tangent) * root_coef * (
        1.0 + 3.0 * cubic_coef * values * values
    )
    return (forward, slopes)


def pick_blocks(slices, pattern, block_size):
    picked = []
    for which_section, source in enumerate(slices):
        shaped = source.reshape(source.shape[0], -1, block_size)
        picked.append(jnp.take(shaped, pattern[:, which_section], axis=1))
    return jnp.stack(picked, axis=2)


def shards(
    inputs, cotangent, up_blocks, down_blocks, low_left, low_right, up_pattern, down_pattern
):
    tokens_here, width_here = inputs.shape
    block_size = up_blocks.shape[3]
    hidden_here = up_blocks.shape[1]
    section_count = up_blocks.shape[2]
    blocks_here = width_here // block_size
    dp_size = lax.axis_size("dp")
    inv_root = 1.0 / math.sqrt(tokens_here * dp_size)
    up_fetched = fetch_share(up_blocks)
    down_fetched = fetch_share(down_blocks)
    up_full = swap_shares(up_fetched, up_blocks)
    sources = [inputs] + [
        swapped(inputs, "tensor", level_bit) for level_bit in range(section_count - 1)
    ]
    selected = pick_blocks(sources, up_pattern, block_size)
    sparse = jnp.einsum("thsi,ihsj->htj", selected, up_full, preferred_element_type=jnp.float32)
    right_blocks = low_right.reshape(low_right.shape[0], hidden_here, block_size)
    low_part = lax.dot_general(
        inputs, low_left, (((1,), (1,)), ((), ())), preferred_element_type=jnp.float32
    )
    low_sum = butterfly_sum(low_part, "tensor").astype(jnp.bfloat16)
    preact = sparse + jnp.einsum(
        "tr,rhj->htj", low_sum, right_blocks, preferred_element_type=jnp.float32
    )
    activated, slopes = gelu_pair(preact)
    hidden = activated.astype(jnp.bfloat16)
    picked = pick_blocks([cotangent] * section_count, down_pattern, block_size)
    down_parts = (
        jnp.stack(
            [
                jnp.einsum("htj,thso->hjso", rows, picked, preferred_element_type=jnp.float32)
                for rows in split_rows(hidden, 2, dp_size)
            ]
        )
        * inv_root
    ).astype(jnp.bfloat16)
    down_parts, down_fetched = lax.optimization_barrier((down_parts, down_fetched))
    down_full = swap_shares(down_fetched, down_blocks)
    down_summed = lax.psum_scatter(down_parts, "dp", scatter_dimension=0, tiled=False)
    grad_hidden = jnp.einsum(
        "thso,jhso->htj", picked, down_full, preferred_element_type=jnp.float32
    )
    grad_blocks = (grad_hidden * slopes).astype(jnp.bfloat16)
    up_parts = jnp.stack(
        [
            jnp.einsum("thsi,htj->hsij", rows, grad_blocks, preferred_element_type=jnp.float32)
            for rows in split_rows(selected, 3, dp_size)
        ]
    )
    slot_ids = jnp.arange(blocks_here, dtype=jnp.int32)

    def section_term(which_section):
        spread = jnp.einsum(
            "htj,ihj->thi",
            grad_blocks,
            up_full[:, :, which_section, :],
            preferred_element_type=jnp.float32,
        )
        placing = (up_pattern[:, which_section][:, None] == slot_ids[None, :]).astype(jnp.float32)
        return jnp.einsum("thi,hd->tdi", spread, placing).reshape(tokens_here, width_here)

    incoming = [
        swapped(section_term(level_bit + 1).astype(jnp.bfloat16), "tensor", level_bit)
        for level_bit in range(section_count - 1)
    ]
    up_parts, down_summed = lax.optimization_barrier(
        ((up_parts * inv_root).astype(jnp.bfloat16), down_summed)
    )
    grad_down = jnp.transpose(down_summed.astype(jnp.float32), (1, 0, 2, 3))
    back_part = jnp.einsum(
        "htj,rhj->tr", grad_blocks, right_blocks, preferred_element_type=jnp.float32
    )
    back_low = butterfly_sum(back_part, "tensor").astype(jnp.bfloat16)
    up_summed = lax.psum_scatter(up_parts, "dp", scatter_dimension=0, tiled=False)
    left_parts = jnp.stack(
        split_rows(
            lax.dot_general(
                back_low, inputs, (((0,), (0,)), ((), ())), preferred_element_type=jnp.float32
            ),
            0,
            dp_size,
        )
    )
    right_parts = jnp.stack(
        split_rows(
            jnp.einsum(
                "tr,htj->rhj", low_sum, grad_blocks, preferred_element_type=jnp.float32
            ).reshape(low_sum.shape[1], -1),
            0,
            dp_size,
        )
    )
    joined = (jnp.concatenate([left_parts, right_parts], axis=2) * inv_root).astype(jnp.bfloat16)
    joined, up_summed, incoming = lax.optimization_barrier((joined, up_summed, incoming))
    joined = lax.psum_scatter(joined, "dp", scatter_dimension=0, tiled=False).astype(jnp.float32)
    grad_up = jnp.transpose(up_summed.astype(jnp.float32), (2, 0, 1, 3))
    own_term = section_term(0)
    for level_bit in range(section_count - 1):
        own_term = own_term + incoming[level_bit].astype(jnp.float32)
    grad_input = (
        own_term + jnp.dot(back_low, low_left, preferred_element_type=jnp.float32)
    ).astype(jnp.bfloat16)
    grad_left = joined[:, :width_here]
    grad_right = joined[:, width_here:]
    return (grad_input, grad_up, grad_down, grad_left, grad_right)


def solution(mesh):
    in_specs = (
        P(("groups", "dp"), "tensor"),
        P(("groups", "dp"), "tensor"),
        P("dp", "tensor", None, None),
        P("dp", "tensor", None, None),
        P(None, "tensor"),
        P(None, "tensor"),
        P("tensor", None),
        P("tensor", None),
    )
    out_specs = (
        P(("groups", "dp"), "tensor"),
        P(("groups", "dp"), "tensor", None, None),
        P(("groups", "dp"), "tensor", None, None),
        P(("groups", "dp"), "tensor"),
        P(("groups", "dp"), "tensor"),
    )
    return jax.shard_map(shards, mesh=mesh, in_specs=in_specs, out_specs=out_specs, check_vma=False)
```

```python
import math

import jax
import jax.numpy as jnp
from jax import lax
from jax.sharding import PartitionSpec as P

root_coef = 0.7978845608028654
cubic_coef = 0.044715


def swapped(block, axis, distance):
    count = lax.axis_size(axis)
    route = []
    for low in range(count):
        high = low | 1 << distance
        if high != low and high < count:
            route += [(low, high), (high, low)]
    return lax.ppermute(block, axis, route)


def fetch_share(block):
    group_count = lax.axis_size("groups")
    rows = block.shape[0]
    if group_count == 1 or rows % group_count:
        return lax.all_gather(block, "dp", axis=0, tiled=True)
    share = rows // group_count
    mine = lax.dynamic_slice_in_dim(block, lax.axis_index("groups") * share, share, axis=0)
    return lax.all_gather(mine, "dp", axis=0, tiled=False)


def rotated(values, start):
    count = values.shape[0]
    doubled = jnp.concatenate([values, values], axis=0)
    return lax.dynamic_slice_in_dim(doubled, start % count, count, axis=0)


def swap_shares(fetched, block):
    group_count = lax.axis_size("groups")
    if group_count == 1 or block.shape[0] % group_count:
        return fetched, None
    group = lax.axis_index("groups")
    other = None
    if group_count == 2:
        count = fetched.shape[0]
        me = lax.axis_index("dp")
        send = rotated(fetched, me + 1)[: count - 1]
        got = lax.ppermute(send, "groups", [(0, 1), (1, 0)])
        share = block.shape[0] // 2
        local = lax.dynamic_slice_in_dim(block, (1 - group) * share, share, axis=0)
        other = rotated(jnp.concatenate([got, local[None]], axis=0), count - 1 - me)
        received = [fetched, other]
    else:
        received = [fetched] + [
            lax.ppermute(
                fetched, "groups", [(g, (g + shift) % group_count) for g in range(group_count)]
            )
            for shift in range(1, group_count)
        ]
    reverse = jnp.stack(received[::-1], axis=1)
    doubled = jnp.concatenate([reverse, reverse], axis=1)
    ordered = lax.dynamic_slice_in_dim(doubled, group_count - 1 - group, group_count, axis=1)
    return ordered.reshape((-1,) + block.shape[1:]), other


def split_rows(values, axis, count):
    rows = values.shape[axis] // count
    return [lax.slice_in_dim(values, d * rows, (d + 1) * rows, axis=axis) for d in range(count)]


def butterfly_sum(values, axis):
    count = lax.axis_size(axis)
    if count & (count - 1):
        return lax.psum(values.astype(jnp.bfloat16), axis).astype(jnp.float32)
    total = values
    distance = 0
    while (1 << distance) < count:
        total = total + swapped(total, axis, distance)
        distance += 1
    return total


def gelu_pair(values):
    inner_arg = root_coef * (values + cubic_coef * values * values * values)
    tangent = jnp.tanh(inner_arg)
    forward = 0.5 * values * (1.0 + tangent)
    slopes = 0.5 * (1.0 + tangent) + 0.5 * values * (1.0 - tangent * tangent) * root_coef * (
        1.0 + 3.0 * cubic_coef * values * values
    )
    return (forward, slopes)


def pick_blocks(slices, pattern, block_size):
    picked = []
    for which_section, source in enumerate(slices):
        shaped = source.reshape(source.shape[0], -1, block_size)
        picked.append(jnp.take(shaped, pattern[:, which_section], axis=1))
    return jnp.stack(picked, axis=2)


def shards(
    inputs, cotangent, up_blocks, down_blocks, low_left, low_right, up_pattern, down_pattern
):
    tokens_here, width_here = inputs.shape
    block_size = up_blocks.shape[3]
    hidden_here = up_blocks.shape[1]
    section_count = up_blocks.shape[2]
    blocks_here = width_here // block_size
    dp_size = lax.axis_size("dp")
    inv_root = 1.0 / math.sqrt(tokens_here * dp_size)
    up_fetched = fetch_share(up_blocks)
    down_fetched = fetch_share(down_blocks)
    up_full, up_other = swap_shares(up_fetched, up_blocks)
    sources = [inputs] + [
        swapped(inputs, "tensor", level_bit) for level_bit in range(section_count - 1)
    ]
    selected = pick_blocks(sources, up_pattern, block_size)
    if up_other is None:
        sparse = jnp.einsum(
            "thsi,ihsj->htj", selected, up_full, preferred_element_type=jnp.float32
        )
    else:
        group = lax.axis_index("groups")
        by_share = selected.reshape(selected.shape[:3] + (dp_size, 2, -1))
        own_rows = lax.dynamic_index_in_dim(by_share, group, 4, keepdims=False)
        other_rows = lax.dynamic_index_in_dim(by_share, 1 - group, 4, keepdims=False)
        sparse = jnp.einsum(
            "thskr,krhsj->htj", own_rows, up_fetched, preferred_element_type=jnp.float32
        ) + jnp.einsum(
            "thskr,krhsj->htj", other_rows, up_other, preferred_element_type=jnp.float32
        )
    right_blocks = low_right.reshape(low_right.shape[0], hidden_here, block_size)
    low_part = lax.dot_general(
        inputs, low_left, (((1,), (1,)), ((), ())), preferred_element_type=jnp.float32
    )
    low_sum = butterfly_sum(low_part, "tensor").astype(jnp.bfloat16)
    preact = sparse + jnp.einsum(
        "tr,rhj->htj", low_sum, right_blocks, preferred_element_type=jnp.float32
    )
    activated, slopes = gelu_pair(preact)
    hidden = activated.astype(jnp.bfloat16)
    picked = pick_blocks([cotangent] * section_count, down_pattern, block_size)
    down_parts = (
        jnp.stack(
            [
                jnp.einsum("htj,thso->hjso", rows, picked, preferred_element_type=jnp.float32)
                for rows in split_rows(hidden, 2, dp_size)
            ]
        )
        * inv_root
    ).astype(jnp.bfloat16)
    down_parts, down_fetched = lax.optimization_barrier((down_parts, down_fetched))
    down_full, _ = swap_shares(down_fetched, down_blocks)
    down_summed = lax.psum_scatter(down_parts, "dp", scatter_dimension=0, tiled=False)
    grad_hidden = jnp.einsum(
        "thso,jhso->htj", picked, down_full, preferred_element_type=jnp.float32
    )
    grad_blocks = (grad_hidden * slopes).astype(jnp.bfloat16)
    up_parts = jnp.stack(
        [
            jnp.einsum("thsi,htj->hsij", rows, grad_blocks, preferred_element_type=jnp.float32)
            for rows in split_rows(selected, 3, dp_size)
        ]
    )
    slot_ids = jnp.arange(blocks_here, dtype=jnp.int32)

    def section_term(which_section):
        spread = jnp.einsum(
            "htj,ihj->thi",
            grad_blocks,
            up_full[:, :, which_section, :],
            preferred_element_type=jnp.float32,
        )
        placing = (up_pattern[:, which_section][:, None] == slot_ids[None, :]).astype(jnp.float32)
        return jnp.einsum("thi,hd->tdi", spread, placing).reshape(tokens_here, width_here)

    incoming = [
        swapped(section_term(level_bit + 1).astype(jnp.bfloat16), "tensor", level_bit)
        for level_bit in range(section_count - 1)
    ]
    up_parts, down_summed = lax.optimization_barrier(
        ((up_parts * inv_root).astype(jnp.bfloat16), down_summed)
    )
    grad_down = jnp.transpose(down_summed.astype(jnp.float32), (1, 0, 2, 3))
    back_part = jnp.einsum(
        "htj,rhj->tr", grad_blocks, right_blocks, preferred_element_type=jnp.float32
    )
    back_low = butterfly_sum(back_part, "tensor").astype(jnp.bfloat16)
    up_summed = lax.psum_scatter(up_parts, "dp", scatter_dimension=0, tiled=False)
    left_parts = jnp.stack(
        split_rows(
            lax.dot_general(
                back_low, inputs, (((0,), (0,)), ((), ())), preferred_element_type=jnp.float32
            ),
            0,
            dp_size,
        )
    )
    right_parts = jnp.stack(
        split_rows(
            jnp.einsum(
                "tr,htj->rhj", low_sum, grad_blocks, preferred_element_type=jnp.float32
            ).reshape(low_sum.shape[1], -1),
            0,
            dp_size,
        )
    )
    joined = (jnp.concatenate([left_parts, right_parts], axis=2) * inv_root).astype(jnp.bfloat16)
    joined, up_summed, incoming = lax.optimization_barrier((joined, up_summed, incoming))
    joined = lax.psum_scatter(joined, "dp", scatter_dimension=0, tiled=False).astype(jnp.float32)
    grad_up = jnp.transpose(up_summed.astype(jnp.float32), (2, 0, 1, 3))
    own_term = section_term(0)
    for level_bit in range(section_count - 1):
        own_term = own_term + incoming[level_bit].astype(jnp.float32)
    grad_input = (
        own_term + jnp.dot(back_low, low_left, preferred_element_type=jnp.float32)
    ).astype(jnp.bfloat16)
    grad_left = joined[:, :width_here]
    grad_right = joined[:, width_here:]
    return (grad_input, grad_up, grad_down, grad_left, grad_right)


def solution(mesh):
    in_specs = (
        P(("groups", "dp"), "tensor"),
        P(("groups", "dp"), "tensor"),
        P("dp", "tensor", None, None),
        P("dp", "tensor", None, None),
        P(None, "tensor"),
        P(None, "tensor"),
        P("tensor", None),
        P("tensor", None),
    )
    out_specs = (
        P(("groups", "dp"), "tensor"),
        P(("groups", "dp"), "tensor", None, None),
        P(("groups", "dp"), "tensor", None, None),
        P(("groups", "dp"), "tensor"),
        P(("groups", "dp"), "tensor"),
    )
    return jax.shard_map(shards, mesh=mesh, in_specs=in_specs, out_specs=out_specs, check_vma=False)
```

```python
import math

import jax
import jax.numpy as jnp
from jax import lax
from jax.sharding import PartitionSpec as P

root_coef = 0.7978845608028654
cubic_coef = 0.044715


def swapped(block, axis, distance):
    count = lax.axis_size(axis)
    route = []
    for low in range(count):
        high = low | 1 << distance
        if high != low and high < count:
            route += [(low, high), (high, low)]
    return lax.ppermute(block, axis, route)


def fetch_share(block):
    group_count = lax.axis_size("groups")
    rows = block.shape[0]
    if group_count == 1 or rows % group_count:
        return lax.all_gather(block, "dp", axis=0, tiled=True)
    share = rows // group_count
    mine = lax.dynamic_slice_in_dim(block, lax.axis_index("groups") * share, share, axis=0)
    return lax.all_gather(mine, "dp", axis=0, tiled=False)


def rotated(values, start):
    count = values.shape[0]
    doubled = jnp.concatenate([values, values], axis=0)
    return lax.dynamic_slice_in_dim(doubled, start % count, count, axis=0)


def swap_shares(fetched, block):
    group_count = lax.axis_size("groups")
    if group_count == 1 or block.shape[0] % group_count:
        return fetched, None
    group = lax.axis_index("groups")
    other = None
    if group_count == 2:
        count = fetched.shape[0]
        me = lax.axis_index("dp")
        send = rotated(fetched, me + 1)[: count - 1]
        share = block.shape[0] // 2
        local = lax.dynamic_slice_in_dim(block, (1 - group) * share, share, axis=0)
        halves = 2 if block.shape[1] % 2 == 0 else 1
        width = block.shape[1] // halves
        other = []
        for half in range(halves):
            got = lax.ppermute(
                send[:, :, half * width : (half + 1) * width], "groups", [(0, 1), (1, 0)]
            )
            piece = jnp.concatenate([got, local[None, :, half * width : (half + 1) * width]], axis=0)
            other.append(rotated(piece, count - 1 - me))
        received = [fetched, jnp.concatenate(other, axis=2)]
    else:
        received = [fetched] + [
            lax.ppermute(
                fetched, "groups", [(g, (g + shift) % group_count) for g in range(group_count)]
            )
            for shift in range(1, group_count)
        ]
    reverse = jnp.stack(received[::-1], axis=1)
    doubled = jnp.concatenate([reverse, reverse], axis=1)
    ordered = lax.dynamic_slice_in_dim(doubled, group_count - 1 - group, group_count, axis=1)
    return ordered.reshape((-1,) + block.shape[1:]), other


def split_rows(values, axis, count):
    rows = values.shape[axis] // count
    return [lax.slice_in_dim(values, d * rows, (d + 1) * rows, axis=axis) for d in range(count)]


def butterfly_sum(values, axis):
    count = lax.axis_size(axis)
    if count & (count - 1):
        return lax.psum(values.astype(jnp.bfloat16), axis).astype(jnp.float32)
    total = values
    distance = 0
    while (1 << distance) < count:
        total = total + swapped(total, axis, distance)
        distance += 1
    return total


def gelu_pair(values):
    inner_arg = root_coef * (values + cubic_coef * values * values * values)
    tangent = jnp.tanh(inner_arg)
    forward = 0.5 * values * (1.0 + tangent)
    slopes = 0.5 * (1.0 + tangent) + 0.5 * values * (1.0 - tangent * tangent) * root_coef * (
        1.0 + 3.0 * cubic_coef * values * values
    )
    return (forward, slopes)


def pick_blocks(slices, pattern, block_size):
    picked = []
    for which_section, source in enumerate(slices):
        shaped = source.reshape(source.shape[0], -1, block_size)
        picked.append(jnp.take(shaped, pattern[:, which_section], axis=1))
    return jnp.stack(picked, axis=2)


def shards(
    inputs, cotangent, up_blocks, down_blocks, low_left, low_right, up_pattern, down_pattern
):
    tokens_here, width_here = inputs.shape
    block_size = up_blocks.shape[3]
    hidden_here = up_blocks.shape[1]
    section_count = up_blocks.shape[2]
    blocks_here = width_here // block_size
    dp_size = lax.axis_size("dp")
    inv_root = 1.0 / math.sqrt(tokens_here * dp_size)
    up_fetched = fetch_share(up_blocks)
    down_fetched = fetch_share(down_blocks)
    up_full, up_other = swap_shares(up_fetched, up_blocks)
    sources = [inputs] + [
        swapped(inputs, "tensor", level_bit) for level_bit in range(section_count - 1)
    ]
    selected = pick_blocks(sources, up_pattern, block_size)
    low_part = lax.dot_general(
        inputs, low_left, (((1,), (1,)), ((), ())), preferred_element_type=jnp.float32
    )
    low_sum = butterfly_sum(low_part, "tensor").astype(jnp.bfloat16)
    right_blocks = low_right.reshape(low_right.shape[0], hidden_here, block_size)
    low_term = jnp.einsum("tr,rhj->htj", low_sum, right_blocks, preferred_element_type=jnp.float32)
    picked = pick_blocks([cotangent] * section_count, down_pattern, block_size)
    if up_other is None:
        sparse = jnp.einsum(
            "thsi,ihsj->htj", selected, up_full, preferred_element_type=jnp.float32
        )
        spans = [(0, hidden_here, sparse)]
    else:
        group = lax.axis_index("groups")
        by_share = selected.reshape(selected.shape[:3] + (dp_size, 2, -1))
        own_rows = lax.dynamic_index_in_dim(by_share, group, 4, keepdims=False)
        other_rows = lax.dynamic_index_in_dim(by_share, 1 - group, 4, keepdims=False)
        own_sum = jnp.einsum(
            "thskr,krhsj->htj", own_rows, up_fetched, preferred_element_type=jnp.float32
        )
        spans = []
        lo = 0
        for piece in up_other:
            hi = lo + piece.shape[2]
            spans.append(
                (
                    lo,
                    hi,
                    own_sum[lo:hi]
                    + jnp.einsum(
                        "thskr,krhsj->htj",
                        other_rows[:, lo:hi],
                        piece,
                        preferred_element_type=jnp.float32,
                    ),
                )
            )
            lo = hi
    hidden_spans, slope_spans, down_spans = [], [], []
    for lo, hi, sparse in spans:
        activated, slopes_here = gelu_pair(sparse + low_term[lo:hi])
        hidden_here_span = activated.astype(jnp.bfloat16)
        hidden_spans.append(hidden_here_span)
        slope_spans.append(slopes_here)
        down_spans.append(
            jnp.stack(
                [
                    jnp.einsum(
                        "htj,thso->hjso", rows, picked[:, lo:hi], preferred_element_type=jnp.float32
                    )
                    for rows in split_rows(hidden_here_span, 2, dp_size)
                ]
            )
        )
    hidden = jnp.concatenate(hidden_spans, axis=0)
    slopes = jnp.concatenate(slope_spans, axis=0)
    down_parts = (jnp.concatenate(down_spans, axis=1) * inv_root).astype(jnp.bfloat16)
    down_parts, down_fetched = lax.optimization_barrier((down_parts, down_fetched))
    down_full, _ = swap_shares(down_fetched, down_blocks)
    down_summed = lax.psum_scatter(down_parts, "dp", scatter_dimension=0, tiled=False)
    grad_hidden = jnp.einsum(
        "thso,jhso->htj", picked, down_full, preferred_element_type=jnp.float32
    )
    grad_blocks = (grad_hidden * slopes).astype(jnp.bfloat16)
    up_parts = jnp.stack(
        [
            jnp.einsum("thsi,htj->hsij", rows, grad_blocks, preferred_element_type=jnp.float32)
            for rows in split_rows(selected, 3, dp_size)
        ]
    )
    slot_ids = jnp.arange(blocks_here, dtype=jnp.int32)

    def section_term(which_section):
        spread = jnp.einsum(
            "htj,ihj->thi",
            grad_blocks,
            up_full[:, :, which_section, :],
            preferred_element_type=jnp.float32,
        )
        placing = (up_pattern[:, which_section][:, None] == slot_ids[None, :]).astype(jnp.float32)
        return jnp.einsum("thi,hd->tdi", spread, placing).reshape(tokens_here, width_here)

    incoming = [
        swapped(section_term(level_bit + 1).astype(jnp.bfloat16), "tensor", level_bit)
        for level_bit in range(section_count - 1)
    ]
    up_parts, down_summed = lax.optimization_barrier(
        ((up_parts * inv_root).astype(jnp.bfloat16), down_summed)
    )
    grad_down = jnp.transpose(down_summed.astype(jnp.float32), (1, 0, 2, 3))
    back_part = jnp.einsum(
        "htj,rhj->tr", grad_blocks, right_blocks, preferred_element_type=jnp.float32
    )
    back_low = butterfly_sum(back_part, "tensor").astype(jnp.bfloat16)
    up_summed = lax.psum_scatter(up_parts, "dp", scatter_dimension=0, tiled=False)
    left_parts = jnp.stack(
        split_rows(
            lax.dot_general(
                back_low, inputs, (((0,), (0,)), ((), ())), preferred_element_type=jnp.float32
            ),
            0,
            dp_size,
        )
    )
    right_parts = jnp.stack(
        split_rows(
            jnp.einsum(
                "tr,htj->rhj", low_sum, grad_blocks, preferred_element_type=jnp.float32
            ).reshape(low_sum.shape[1], -1),
            0,
            dp_size,
        )
    )
    joined = (jnp.concatenate([left_parts, right_parts], axis=2) * inv_root).astype(jnp.bfloat16)
    joined, up_summed, incoming = lax.optimization_barrier((joined, up_summed, incoming))
    joined = lax.psum_scatter(joined, "dp", scatter_dimension=0, tiled=False).astype(jnp.float32)
    grad_up = jnp.transpose(up_summed.astype(jnp.float32), (2, 0, 1, 3))
    own_term = section_term(0)
    for level_bit in range(section_count - 1):
        own_term = own_term + incoming[level_bit].astype(jnp.float32)
    grad_input = (
        own_term + jnp.dot(back_low, low_left, preferred_element_type=jnp.float32)
    ).astype(jnp.bfloat16)
    grad_left = joined[:, :width_here]
    grad_right = joined[:, width_here:]
    return (grad_input, grad_up, grad_down, grad_left, grad_right)


def solution(mesh):
    in_specs = (
        P(("groups", "dp"), "tensor"),
        P(("groups", "dp"), "tensor"),
        P("dp", "tensor", None, None),
        P("dp", "tensor", None, None),
        P(None, "tensor"),
        P(None, "tensor"),
        P("tensor", None),
        P("tensor", None),
    )
    out_specs = (
        P(("groups", "dp"), "tensor"),
        P(("groups", "dp"), "tensor", None, None),
        P(("groups", "dp"), "tensor", None, None),
        P(("groups", "dp"), "tensor"),
        P(("groups", "dp"), "tensor"),
    )
    return jax.shard_map(shards, mesh=mesh, in_specs=in_specs, out_specs=out_specs, check_vma=False)
```

```python
import math

import jax
import jax.numpy as jnp
from jax import lax
from jax.sharding import PartitionSpec as P

root_coef = 0.7978845608028654
cubic_coef = 0.044715


def swapped(block, axis, distance):
    count = lax.axis_size(axis)
    route = []
    for low in range(count):
        high = low | 1 << distance
        if high != low and high < count:
            route += [(low, high), (high, low)]
    return lax.ppermute(block, axis, route)


def fetch_share(block):
    group_count = lax.axis_size("groups")
    rows = block.shape[0]
    if group_count == 1 or rows % group_count:
        return lax.all_gather(block, "dp", axis=0, tiled=True)
    share = rows // group_count
    mine = lax.dynamic_slice_in_dim(block, lax.axis_index("groups") * share, share, axis=0)
    return lax.all_gather(mine, "dp", axis=0, tiled=False)


def rotated(values, start):
    count = values.shape[0]
    doubled = jnp.concatenate([values, values], axis=0)
    return lax.dynamic_slice_in_dim(doubled, start % count, count, axis=0)


def swap_shares(fetched, block):
    group_count = lax.axis_size("groups")
    if group_count == 1 or block.shape[0] % group_count:
        return fetched, None
    group = lax.axis_index("groups")
    other = None
    if group_count == 2:
        count = fetched.shape[0]
        me = lax.axis_index("dp")
        send = rotated(fetched, me + 1)[: count - 1]
        share = block.shape[0] // 2
        local = lax.dynamic_slice_in_dim(block, (1 - group) * share, share, axis=0)
        halves = 4 if block.shape[1] % 4 == 0 else 1
        width = block.shape[1] // halves
        other = []
        for half in range(halves):
            got = lax.ppermute(
                send[:, :, half * width : (half + 1) * width], "groups", [(0, 1), (1, 0)]
            )
            piece = jnp.concatenate([got, local[None, :, half * width : (half + 1) * width]], axis=0)
            other.append(rotated(piece, count - 1 - me))
        received = [fetched, jnp.concatenate(other, axis=2)]
    else:
        received = [fetched] + [
            lax.ppermute(
                fetched, "groups", [(g, (g + shift) % group_count) for g in range(group_count)]
            )
            for shift in range(1, group_count)
        ]
    reverse = jnp.stack(received[::-1], axis=1)
    doubled = jnp.concatenate([reverse, reverse], axis=1)
    ordered = lax.dynamic_slice_in_dim(doubled, group_count - 1 - group, group_count, axis=1)
    return ordered.reshape((-1,) + block.shape[1:]), other


def split_rows(values, axis, count):
    rows = values.shape[axis] // count
    return [lax.slice_in_dim(values, d * rows, (d + 1) * rows, axis=axis) for d in range(count)]


def butterfly_sum(values, axis):
    count = lax.axis_size(axis)
    if count & (count - 1):
        return lax.psum(values.astype(jnp.bfloat16), axis).astype(jnp.float32)
    total = values
    distance = 0
    while (1 << distance) < count:
        total = total + swapped(total, axis, distance)
        distance += 1
    return total


def gelu_pair(values):
    inner_arg = root_coef * (values + cubic_coef * values * values * values)
    tangent = jnp.tanh(inner_arg)
    forward = 0.5 * values * (1.0 + tangent)
    slopes = 0.5 * (1.0 + tangent) + 0.5 * values * (1.0 - tangent * tangent) * root_coef * (
        1.0 + 3.0 * cubic_coef * values * values
    )
    return (forward, slopes)


def pick_blocks(slices, pattern, block_size):
    picked = []
    for which_section, source in enumerate(slices):
        shaped = source.reshape(source.shape[0], -1, block_size)
        picked.append(jnp.take(shaped, pattern[:, which_section], axis=1))
    return jnp.stack(picked, axis=2)


def shards(
    inputs, cotangent, up_blocks, down_blocks, low_left, low_right, up_pattern, down_pattern
):
    tokens_here, width_here = inputs.shape
    block_size = up_blocks.shape[3]
    hidden_here = up_blocks.shape[1]
    section_count = up_blocks.shape[2]
    blocks_here = width_here // block_size
    dp_size = lax.axis_size("dp")
    inv_root = 1.0 / math.sqrt(tokens_here * dp_size)
    up_fetched = fetch_share(up_blocks)
    down_fetched = fetch_share(down_blocks)
    up_full, up_other = swap_shares(up_fetched, up_blocks)
    sources = [inputs] + [
        swapped(inputs, "tensor", level_bit) for level_bit in range(section_count - 1)
    ]
    selected = pick_blocks(sources, up_pattern, block_size)
    low_part = lax.dot_general(
        inputs, low_left, (((1,), (1,)), ((), ())), preferred_element_type=jnp.float32
    )
    low_sum = butterfly_sum(low_part, "tensor").astype(jnp.bfloat16)
    right_blocks = low_right.reshape(low_right.shape[0], hidden_here, block_size)
    low_term = jnp.einsum("tr,rhj->htj", low_sum, right_blocks, preferred_element_type=jnp.float32)
    picked = pick_blocks([cotangent] * section_count, down_pattern, block_size)
    if up_other is None:
        sparse = jnp.einsum(
            "thsi,ihsj->htj", selected, up_full, preferred_element_type=jnp.float32
        )
        spans = [(0, hidden_here, sparse)]
    else:
        group = lax.axis_index("groups")
        by_share = selected.reshape(selected.shape[:3] + (dp_size, 2, -1))
        own_rows = lax.dynamic_index_in_dim(by_share, group, 4, keepdims=False)
        other_rows = lax.dynamic_index_in_dim(by_share, 1 - group, 4, keepdims=False)
        own_sum = jnp.einsum(
            "thskr,krhsj->htj", own_rows, up_fetched, preferred_element_type=jnp.float32
        )
        spans = []
        lo = 0
        for piece in up_other:
            hi = lo + piece.shape[2]
            spans.append(
                (
                    lo,
                    hi,
                    own_sum[lo:hi]
                    + jnp.einsum(
                        "thskr,krhsj->htj",
                        other_rows[:, lo:hi],
                        piece,
                        preferred_element_type=jnp.float32,
                    ),
                )
            )
            lo = hi
    hidden_spans, slope_spans, down_spans = [], [], []
    for lo, hi, sparse in spans:
        activated, slopes_here = gelu_pair(sparse + low_term[lo:hi])
        hidden_here_span = activated.astype(jnp.bfloat16)
        hidden_spans.append(hidden_here_span)
        slope_spans.append(slopes_here)
        down_spans.append(
            jnp.stack(
                [
                    jnp.einsum(
                        "htj,thso->hjso", rows, picked[:, lo:hi], preferred_element_type=jnp.float32
                    )
                    for rows in split_rows(hidden_here_span, 2, dp_size)
                ]
            )
        )
    hidden = jnp.concatenate(hidden_spans, axis=0)
    slopes = jnp.concatenate(slope_spans, axis=0)
    down_parts = (jnp.concatenate(down_spans, axis=1) * inv_root).astype(jnp.bfloat16)
    down_parts, down_fetched = lax.optimization_barrier((down_parts, down_fetched))
    down_full, _ = swap_shares(down_fetched, down_blocks)
    down_summed = lax.psum_scatter(down_parts, "dp", scatter_dimension=0, tiled=False)
    grad_hidden = jnp.einsum(
        "thso,jhso->htj", picked, down_full, preferred_element_type=jnp.float32
    )
    grad_blocks = (grad_hidden * slopes).astype(jnp.bfloat16)
    up_parts = jnp.stack(
        [
            jnp.einsum("thsi,htj->hsij", rows, grad_blocks, preferred_element_type=jnp.float32)
            for rows in split_rows(selected, 3, dp_size)
        ]
    )
    slot_ids = jnp.arange(blocks_here, dtype=jnp.int32)

    def section_term(which_section):
        spread = jnp.einsum(
            "htj,ihj->thi",
            grad_blocks,
            up_full[:, :, which_section, :],
            preferred_element_type=jnp.float32,
        )
        placing = (up_pattern[:, which_section][:, None] == slot_ids[None, :]).astype(jnp.float32)
        return jnp.einsum("thi,hd->tdi", spread, placing).reshape(tokens_here, width_here)

    incoming = [
        swapped(section_term(level_bit + 1).astype(jnp.bfloat16), "tensor", level_bit)
        for level_bit in range(section_count - 1)
    ]
    up_parts, down_summed = lax.optimization_barrier(
        ((up_parts * inv_root).astype(jnp.bfloat16), down_summed)
    )
    grad_down = jnp.transpose(down_summed.astype(jnp.float32), (1, 0, 2, 3))
    back_part = jnp.einsum(
        "htj,rhj->tr", grad_blocks, right_blocks, preferred_element_type=jnp.float32
    )
    back_low = butterfly_sum(back_part, "tensor").astype(jnp.bfloat16)
    up_summed = lax.psum_scatter(up_parts, "dp", scatter_dimension=0, tiled=False)
    left_parts = jnp.stack(
        split_rows(
            lax.dot_general(
                back_low, inputs, (((0,), (0,)), ((), ())), preferred_element_type=jnp.float32
            ),
            0,
            dp_size,
        )
    )
    right_parts = jnp.stack(
        split_rows(
            jnp.einsum(
                "tr,htj->rhj", low_sum, grad_blocks, preferred_element_type=jnp.float32
            ).reshape(low_sum.shape[1], -1),
            0,
            dp_size,
        )
    )
    joined = (jnp.concatenate([left_parts, right_parts], axis=2) * inv_root).astype(jnp.bfloat16)
    joined, up_summed, incoming = lax.optimization_barrier((joined, up_summed, incoming))
    joined = lax.psum_scatter(joined, "dp", scatter_dimension=0, tiled=False).astype(jnp.float32)
    grad_up = jnp.transpose(up_summed.astype(jnp.float32), (2, 0, 1, 3))
    own_term = section_term(0)
    for level_bit in range(section_count - 1):
        own_term = own_term + incoming[level_bit].astype(jnp.float32)
    grad_input = (
        own_term + jnp.dot(back_low, low_left, preferred_element_type=jnp.float32)
    ).astype(jnp.bfloat16)
    grad_left = joined[:, :width_here]
    grad_right = joined[:, width_here:]
    return (grad_input, grad_up, grad_down, grad_left, grad_right)


def solution(mesh):
    in_specs = (
        P(("groups", "dp"), "tensor"),
        P(("groups", "dp"), "tensor"),
        P("dp", "tensor", None, None),
        P("dp", "tensor", None, None),
        P(None, "tensor"),
        P(None, "tensor"),
        P("tensor", None),
        P("tensor", None),
    )
    out_specs = (
        P(("groups", "dp"), "tensor"),
        P(("groups", "dp"), "tensor", None, None),
        P(("groups", "dp"), "tensor", None, None),
        P(("groups", "dp"), "tensor"),
        P(("groups", "dp"), "tensor"),
    )
    return jax.shard_map(shards, mesh=mesh, in_specs=in_specs, out_specs=out_specs, check_vma=False)
```

```python
import math

import jax
import jax.numpy as jnp
from jax import lax
from jax.sharding import PartitionSpec as P

root_coef = 0.7978845608028654
cubic_coef = 0.044715


def swapped(block, axis, distance):
    count = lax.axis_size(axis)
    route = []
    for low in range(count):
        high = low | 1 << distance
        if high != low and high < count:
            route += [(low, high), (high, low)]
    return lax.ppermute(block, axis, route)


def fetch_share(block):
    group_count = lax.axis_size("groups")
    rows = block.shape[0]
    if group_count == 1 or rows % group_count:
        return lax.all_gather(block, "dp", axis=0, tiled=True)
    share = rows // group_count
    mine = lax.dynamic_slice_in_dim(block, lax.axis_index("groups") * share, share, axis=0)
    return lax.all_gather(mine, "dp", axis=0, tiled=False)


def rotated(values, start):
    count = values.shape[0]
    doubled = jnp.concatenate([values, values], axis=0)
    return lax.dynamic_slice_in_dim(doubled, start % count, count, axis=0)


def swap_shares(fetched, block):
    group_count = lax.axis_size("groups")
    if group_count == 1 or block.shape[0] % group_count:
        return fetched, None
    group = lax.axis_index("groups")
    other = None
    if group_count == 2:
        count = fetched.shape[0]
        me = lax.axis_index("dp")
        send = rotated(fetched, me + 1)[: count - 1]
        share = block.shape[0] // 2
        local = lax.dynamic_slice_in_dim(block, (1 - group) * share, share, axis=0)
        halves = 2 if block.shape[1] % 2 == 0 else 1
        width = block.shape[1] // halves
        other = []
        for half in range(halves):
            got = lax.ppermute(
                send[:, :, half * width : (half + 1) * width], "groups", [(0, 1), (1, 0)]
            )
            piece = jnp.concatenate([got, local[None, :, half * width : (half + 1) * width]], axis=0)
            other.append(rotated(piece, count - 1 - me))
        received = [fetched, jnp.concatenate(other, axis=2)]
    else:
        received = [fetched] + [
            lax.ppermute(
                fetched, "groups", [(g, (g + shift) % group_count) for g in range(group_count)]
            )
            for shift in range(1, group_count)
        ]
    reverse = jnp.stack(received[::-1], axis=1)
    doubled = jnp.concatenate([reverse, reverse], axis=1)
    ordered = lax.dynamic_slice_in_dim(doubled, group_count - 1 - group, group_count, axis=1)
    return ordered.reshape((-1,) + block.shape[1:]), other


def split_rows(values, axis, count):
    rows = values.shape[axis] // count
    return [lax.slice_in_dim(values, d * rows, (d + 1) * rows, axis=axis) for d in range(count)]


def butterfly_sum(values, axis):
    count = lax.axis_size(axis)
    if count & (count - 1):
        return lax.psum(values.astype(jnp.bfloat16), axis).astype(jnp.float32)
    total = values
    distance = 0
    while (1 << distance) < count:
        total = total + swapped(total, axis, distance)
        distance += 1
    return total


def gelu_pair(values):
    inner_arg = root_coef * (values + cubic_coef * values * values * values)
    tangent = jnp.tanh(inner_arg)
    forward = 0.5 * values * (1.0 + tangent)
    slopes = 0.5 * (1.0 + tangent) + 0.5 * values * (1.0 - tangent * tangent) * root_coef * (
        1.0 + 3.0 * cubic_coef * values * values
    )
    return (forward, slopes)


def pick_blocks(slices, pattern, block_size):
    picked = []
    for which_section, source in enumerate(slices):
        shaped = source.reshape(source.shape[0], -1, block_size)
        picked.append(jnp.take(shaped, pattern[:, which_section], axis=1))
    return jnp.stack(picked, axis=2)


def shards(
    inputs, cotangent, up_blocks, down_blocks, low_left, low_right, up_pattern, down_pattern
):
    tokens_here, width_here = inputs.shape
    block_size = up_blocks.shape[3]
    hidden_here = up_blocks.shape[1]
    section_count = up_blocks.shape[2]
    blocks_here = width_here // block_size
    dp_size = lax.axis_size("dp")
    inv_root = 1.0 / math.sqrt(tokens_here * dp_size)
    up_fetched = fetch_share(up_blocks)
    down_fetched = fetch_share(down_blocks)
    up_full, up_other = swap_shares(up_fetched, up_blocks)
    sources = [inputs] + [
        swapped(inputs, "tensor", level_bit) for level_bit in range(section_count - 1)
    ]
    selected = pick_blocks(sources, up_pattern, block_size)
    low_part = lax.dot_general(
        inputs, low_left, (((1,), (1,)), ((), ())), preferred_element_type=jnp.float32
    )
    low_sum = butterfly_sum(low_part, "tensor").astype(jnp.bfloat16)
    right_blocks = low_right.reshape(low_right.shape[0], hidden_here, block_size)
    low_term = jnp.einsum("tr,rhj->htj", low_sum, right_blocks, preferred_element_type=jnp.float32)
    picked = pick_blocks([cotangent] * section_count, down_pattern, block_size)
    if up_other is None:
        sparse = jnp.einsum(
            "thsi,ihsj->htj", selected, up_full, preferred_element_type=jnp.float32
        )
        spans = [(0, hidden_here, sparse)]
    else:
        group = lax.axis_index("groups")
        by_share = selected.reshape(selected.shape[:3] + (dp_size, 2, -1))
        own_rows = lax.dynamic_index_in_dim(by_share, group, 4, keepdims=False)
        other_rows = lax.dynamic_index_in_dim(by_share, 1 - group, 4, keepdims=False)
        own_sum = jnp.einsum(
            "thskr,krhsj->htj", own_rows, up_fetched, preferred_element_type=jnp.float32
        )
        spans = []
        lo = 0
        for piece in up_other:
            hi = lo + piece.shape[2]
            spans.append(
                (
                    lo,
                    hi,
                    own_sum[lo:hi]
                    + jnp.einsum(
                        "thskr,krhsj->htj",
                        other_rows[:, lo:hi],
                        piece,
                        preferred_element_type=jnp.float32,
                    ),
                )
            )
            lo = hi
    hidden_spans, slope_spans, down_spans = [], [], []
    for lo, hi, sparse in spans:
        activated, slopes_here = gelu_pair(sparse + low_term[lo:hi])
        hidden_here_span = activated.astype(jnp.bfloat16)
        hidden_spans.append(hidden_here_span)
        slope_spans.append(slopes_here)
        down_spans.append(
            jnp.stack(
                [
                    jnp.einsum(
                        "htj,thso->hjso", rows, picked[:, lo:hi], preferred_element_type=jnp.float32
                    )
                    for rows in split_rows(hidden_here_span, 2, dp_size)
                ]
            )
        )
    hidden = jnp.concatenate(hidden_spans, axis=0)
    slopes = jnp.concatenate(slope_spans, axis=0)
    down_parts = (jnp.concatenate(down_spans, axis=1) * inv_root).astype(jnp.bfloat16)
    down_parts, down_fetched = lax.optimization_barrier((down_parts, down_fetched))
    down_full, _ = swap_shares(down_fetched, down_blocks)
    down_summed = lax.psum_scatter(down_parts, "dp", scatter_dimension=0, tiled=False)
    grad_hidden = jnp.einsum(
        "thso,jhso->htj", picked, down_full, preferred_element_type=jnp.float32
    )
    grad_blocks = (grad_hidden * slopes).astype(jnp.bfloat16)
    up_parts = jnp.stack(
        [
            jnp.einsum("thsi,htj->hsij", rows, grad_blocks, preferred_element_type=jnp.float32)
            for rows in split_rows(selected, 3, dp_size)
        ]
    )
    slot_ids = jnp.arange(blocks_here, dtype=jnp.int32)

    def section_term(which_section):
        spread = jnp.einsum(
            "htj,ihj->thi",
            grad_blocks,
            up_full[:, :, which_section, :],
            preferred_element_type=jnp.float32,
        )
        placing = (up_pattern[:, which_section][:, None] == slot_ids[None, :]).astype(jnp.float32)
        return jnp.einsum("thi,hd->tdi", spread, placing).reshape(tokens_here, width_here)

    incoming = [
        swapped(section_term(level_bit + 1).astype(jnp.bfloat16), "tensor", level_bit)
        for level_bit in range(section_count - 1)
    ]
    up_parts, down_summed = lax.optimization_barrier(
        ((up_parts * inv_root).astype(jnp.bfloat16), down_summed)
    )
    grad_down = jnp.transpose(down_summed.astype(jnp.float32), (1, 0, 2, 3))
    back_part = jnp.einsum(
        "htj,rhj->tr", grad_blocks, right_blocks, preferred_element_type=jnp.float32
    )
    back_low = butterfly_sum(back_part, "tensor").astype(jnp.bfloat16)
    left_parts = jnp.stack(
        split_rows(
            lax.dot_general(
                back_low, inputs, (((0,), (0,)), ((), ())), preferred_element_type=jnp.float32
            ),
            0,
            dp_size,
        )
    )
    right_parts = jnp.stack(
        split_rows(
            jnp.einsum(
                "tr,htj->rhj", low_sum, grad_blocks, preferred_element_type=jnp.float32
            ).reshape(low_sum.shape[1], -1),
            0,
            dp_size,
        )
    )
    joined = (jnp.concatenate([left_parts, right_parts], axis=2) * inv_root).astype(jnp.bfloat16)
    lane = up_parts.shape[-1]
    both = jnp.concatenate(
        [up_parts.reshape(dp_size, -1, lane), joined.reshape(dp_size, -1, lane)], axis=1
    )
    both = lax.psum_scatter(both, "dp", scatter_dimension=0, tiled=False)
    up_size = math.prod(up_parts.shape[1:]) // lane
    up_summed = both[:up_size].reshape(up_parts.shape[1:])
    joined = both[up_size:].reshape(joined.shape[1:]).astype(jnp.float32)
    grad_up = jnp.transpose(up_summed.astype(jnp.float32), (2, 0, 1, 3))
    own_term = section_term(0)
    for level_bit in range(section_count - 1):
        own_term = own_term + incoming[level_bit].astype(jnp.float32)
    grad_input = (
        own_term + jnp.dot(back_low, low_left, preferred_element_type=jnp.float32)
    ).astype(jnp.bfloat16)
    grad_left = joined[:, :width_here]
    grad_right = joined[:, width_here:]
    return (grad_input, grad_up, grad_down, grad_left, grad_right)


def solution(mesh):
    in_specs = (
        P(("groups", "dp"), "tensor"),
        P(("groups", "dp"), "tensor"),
        P("dp", "tensor", None, None),
        P("dp", "tensor", None, None),
        P(None, "tensor"),
        P(None, "tensor"),
        P("tensor", None),
        P("tensor", None),
    )
    out_specs = (
        P(("groups", "dp"), "tensor"),
        P(("groups", "dp"), "tensor", None, None),
        P(("groups", "dp"), "tensor", None, None),
        P(("groups", "dp"), "tensor"),
        P(("groups", "dp"), "tensor"),
    )
    return jax.shard_map(shards, mesh=mesh, in_specs=in_specs, out_specs=out_specs, check_vma=False)
```
